32 devices in a mesh: blk: 8 (over z, core), tp: 4 (over y, x).
Axes of the slice: x: 2, y: 2, z: 4, core: 2. Of those that a mesh axis runs over, the one named last changes fastest.
Arguments:
- tokens: bfloat16 [2048, 5120], P('blk', 'tp'), may hold values from -31 to 31
- norm_gain: bfloat16 [5120], P('tp'), may hold values from 0.15 to 2
- w_query: bfloat16 [5120, 5120], P(None, 'tp'), may hold values from -0.078125 to 0.078125
- w_key: bfloat16 [5120, 1024], P(None, 'tp'), may hold values from -0.078125 to 0.078125
- w_value: bfloat16 [5120, 1024], P(None, 'tp'), may hold values from -0.078125 to 0.078125
- query_bias: bfloat16 [5120], P('tp'), may hold values from -45 to 45
- key_bias: bfloat16 [1024], P('tp'), may hold values from -45 to 45
- value_bias: bfloat16 [1024], P('tp'), may hold values from -4 to 4
- lengths: int32 [8], replicated, may hold values from 1 to 1024, 2048 in all
- page_table: int32 [16], replicated, may hold values from 0 to 15, as said below
Outputs:
- attended: bfloat16 [2048, 5120], P('blk', 'tp')
- kv_cache: bfloat16 [16, 2, 128, 1024], P('blk', None, None, 'tp')
The draws below stay inside these ranges and needn't reach their ends.
Inputs may be any that keep to these rules, and one draw needn't show every extreme that they name: `lengths`: the last piece is padding; the others are prompts. `page_table`: A permutation of the 16 slots; slot s belongs to index s // 2 of blk.
All inputs are finite; a program needn't handle non-finite values.
Results may differ from the reference program's by a relative error of at most 0.012.
The reference program's roundings to bfloat16 on the way (of `scaled` and `weights`) count: a program that leaves them out, or rounds other values in their place, can miss the bound.
Values may be sent and summed in bfloat16 or wider, within the bound.
No kernel may reach another device: no remote copies, remote signals or barrier semaphores. Data moves between devices by JAX's collectives and lax.ppermute only.
A program may use at most 128 MiB of HBM per device.

```python
import math
import jax
import jax.numpy as jnp
import numpy as np
from jax import lax

D = 5120
HEADS = 40
KV_HEADS = 8
HEAD = 128
PAGE = 128
DOCS = 8
STREAM = 2048
PAGES = 16
PAGES_DEV = 2


def column_profile(key, width, offset_tag, lowest, highest):
    along = jnp.arange(width, dtype=jnp.float32) / float(max(width - 1, 1))
    flips = jax.random.randint(jax.random.fold_in(key, 77), (), 0, 2)
    direction = jnp.where(flips == 1, 1.0, -1.0)
    amps = jax.random.uniform(jax.random.fold_in(key, offset_tag), (3,), jnp.float32, 0.5, 1.0)
    phases = jax.random.uniform(jax.random.fold_in(key, offset_tag + 1), (3,), jnp.float32, 0.0, 2.0 * math.pi)
    modes = amps[0] * jnp.sin(2.0 * math.pi * along + phases[0])
    modes = modes + amps[1] * jnp.sin(4.0 * math.pi * along + phases[1])
    modes = modes + amps[2] * jnp.sin(6.0 * math.pi * along + phases[2])
    level = jnp.clip(0.75 * direction * (2.0 * along - 1.0) + 0.25 * modes, -1.0, 1.0)
    low_log = math.log(lowest)
    high_log = math.log(highest)
    return jnp.exp(low_log + (high_log - low_log) * (level + 1.0) * 0.5)


def draw_tokens(key, part):
    profile = column_profile(key, D, 41, 0.35, 3.5)
    jitter = jax.random.uniform(jax.random.fold_in(key, 43), (D,), jnp.float32, 0.75, 1.25)
    base = jnp.clip(jax.random.normal(jax.random.fold_in(key, 44), (STREAM, D), jnp.float32), -4.0, 4.0)
    return (base * (profile * jitter)[None, :]).astype(jnp.bfloat16)


def draw_norm_gain(key, part):
    profile = column_profile(key, D, 51, 0.2, 1.6)
    jitter = jax.random.uniform(jax.random.fold_in(key, 53), (D,), jnp.float32, 0.8, 1.2)
    return (profile * jitter).astype(jnp.bfloat16)


def draw_query_bias(key, part):
    width = HEADS * HEAD
    base = jnp.clip(jax.random.normal(jax.random.fold_in(key, 11), (width,), jnp.float32), -4.0, 4.0)
    return base.astype(jnp.bfloat16)


def draw_key_bias(key, part):
    width = KV_HEADS * HEAD
    base = jnp.clip(jax.random.normal(jax.random.fold_in(key, 21), (width,), jnp.float32), -4.0, 4.0)
    return base.astype(jnp.bfloat16)


def draw_page_table(key, part):
    blocks = PAGES // PAGES_DEV
    owners = jax.random.permutation(jax.random.fold_in(key, 31), blocks)
    within = jax.vmap(lambda sub: jax.random.permutation(sub, PAGES_DEV))(jax.random.split(jax.random.fold_in(key, 32), blocks))
    base = owners[:, None] * PAGES_DEV + within
    flip = jax.random.randint(jax.random.fold_in(key, 33), (blocks // 2,), 0, 2)
    flip_dev = jnp.repeat(flip, 2)
    partner = base.reshape(blocks // 2, 2, PAGES_DEV)[:, ::-1, :].reshape(blocks, PAGES_DEV)
    upper = jnp.arange(PAGES_DEV) >= PAGES_DEV // 2
    final = jnp.where((flip_dev[:, None] == 1) & upper[None, :], partner, base)
    return final.reshape(PAGES).astype(jnp.int32)


def steps_of(stream_key, shape, shards, least, high):
    level, own = 1.0, jax.random.fold_in(stream_key, 6)
    for position, blocks in shards:
        steps = jnp.exp(jax.random.uniform(jax.random.fold_in(own, position), (blocks,), jnp.float32, least / len(shards), high / len(shards)))
        level = level * jnp.repeat(steps, shape[position] // blocks).reshape([-1 if axis == position else 1 for axis in range(len(shape))])
    return level


def length_profile(count, total, reach, skew):
    loads = [(1 << 20) // math.isqrt(rank ** skew) + 1 for rank in range(2, count + 1)]
    surplus, holding = total - reach - (count - 1), [1] * (count - 1)
    while surplus > 0:
        movable = [i for i in range(count - 1) if holding[i] < reach]
        whole, budget = sum([loads[i] for i in movable]), surplus
        for i in movable:
            more = min(reach - holding[i], max(1, budget * loads[i] // whole), surplus)
            holding[i] = holding[i] + more
            surplus = surplus - more
    return np.array([reach] + holding)


def ragged(rng, number_of, total, most, slope):
    if number_of == 2:
        one = jax.random.randint(rng, (), max(1, total - most), min(most, total - 1) + 1)
        return jnp.stack([one, total - one])
    sizes = jnp.asarray(length_profile(number_of, total, most, slope), jnp.int32)
    twos = (number_of - 1) // 2
    donor, receiver = sizes[1:1 + 2 * twos:2], sizes[2:2 + 2 * twos:2]
    room = jnp.minimum(donor - 1, most - receiver)
    moved = jax.random.randint(jax.random.fold_in(rng, 1), (twos,), 0, 1 << 20) % (room + 1)
    sizes = sizes.at[1:1 + 2 * twos:2].set(donor - moved).at[2:2 + 2 * twos:2].set(receiver + moved)
    return sizes[jax.random.permutation(jax.random.fold_in(rng, 2), number_of)]


def centred(rng, shape, scale, limit, shards=(), held_as=jnp.bfloat16):
    values = jax.random.normal(rng, shape, jnp.float32) * scale
    if len(shards) > 0:
        values = steps_of(rng, shape, shards, -0.22, 0.18) * values
    return jnp.clip(values, min=-limit, max=limit).astype(held_as)


def setup_inputs(seed: int = 0) -> dict:
    splits = jax.random.split(jax.random.key(seed), 11)
    tokens = draw_tokens(jax.random.fold_in(splits[10], 71), 0)
    norm_gain = draw_norm_gain(jax.random.fold_in(splits[10], 71), 0)
    w_query = centred(splits[2], (D, HEADS * HEAD), D ** -0.5, 0.078125, ((1, 4),))
    w_key = centred(splits[3], (D, KV_HEADS * HEAD), D ** -0.5, 0.078125, ((1, 4),))
    w_value = centred(splits[4], (D, KV_HEADS * HEAD), D ** -0.5, 0.078125, ((1, 4),))
    query_bias = draw_query_bias(jax.random.fold_in(splits[10], 71), 0)
    key_bias = draw_key_bias(jax.random.fold_in(splits[10], 71), 0)
    value_bias = centred(splits[7], (KV_HEADS * HEAD,), 1.0, 4.0, ((0, 4),))
    lengths = ragged(splits[8], DOCS, STREAM, STREAM // 2, 2).astype(jnp.int32)
    page_table = draw_page_table(jax.random.fold_in(splits[10], 71), 0)
    return {"tokens": tokens, "norm_gain": norm_gain, "w_query": w_query, "w_key": w_key, "w_value": w_value, "query_bias": query_bias, "key_bias": key_bias, "value_bias": value_bias, "lengths": lengths, "page_table": page_table}


rope_base = 1000000.0
norm_eps = 1e-06
neg_large = -1e+30

def token_meta(positions, lengths):
    ends = jnp.cumsum(lengths).astype(jnp.int32)
    past = (positions[:, None] >= ends[None, :]).astype(jnp.int32)
    segment = lax.optimization_barrier(jnp.sum(past, axis=1)).astype(jnp.int32)
    start = lax.optimization_barrier(jnp.sum(past * lengths[None, :], axis=1)).astype(jnp.int32)
    return (segment, positions - start)

def rotate(values, offsets):
    half = HEAD // 2
    freq = rope_base ** (-2.0 * jnp.arange(half, dtype=jnp.float32) / HEAD)
    angle = offsets.astype(jnp.float32)[:, None] * freq[None, :]
    cosine = jnp.cos(angle)[:, None, :]
    sine = jnp.sin(angle)[:, None, :]
    first = values[..., :half]
    second = values[..., half:]
    return jnp.concatenate([first * cosine - second * sine, second * cosine + first * sine], axis=-1)

def reference(tokens, norm_gain, w_query, w_key, w_value, query_bias, key_bias, value_bias, lengths, page_table):
    stream = tokens.shape[0]
    positions = jnp.arange(stream, dtype=jnp.int32)
    segment, offsets = token_meta(positions, lengths)
    live = segment < DOCS - 1
    wide = tokens.astype(jnp.float32)
    rstd = lax.rsqrt(lax.optimization_barrier(jnp.sum(wide * wide, axis=1)) / D + norm_eps)
    scaled = (wide * norm_gain.astype(jnp.float32)).astype(jnp.bfloat16)
    query = rstd[:, None] * jnp.dot(scaled, w_query, preferred_element_type=jnp.float32) + query_bias.astype(jnp.float32)
    key = rstd[:, None] * jnp.dot(scaled, w_key, preferred_element_type=jnp.float32) + key_bias.astype(jnp.float32)
    value = rstd[:, None] * jnp.dot(scaled, w_value, preferred_element_type=jnp.float32) + value_bias.astype(jnp.float32)
    query = rotate(query.reshape(stream, HEADS, HEAD), offsets).astype(jnp.bfloat16)
    key = jnp.where(live[:, None, None], rotate(key.reshape(stream, KV_HEADS, HEAD), offsets), 0.0).astype(jnp.bfloat16)
    value = jnp.where(live[:, None], value, 0.0).astype(jnp.bfloat16).reshape(stream, KV_HEADS, HEAD)
    group = HEADS // KV_HEADS
    block = min(512, stream)
    scale = 1.0 / math_sqrt(HEAD)
    keys_wide = key.astype(jnp.float32)
    values_wide = value.astype(jnp.float32)

    def one_block(index):
        first = index * block
        q_blk = lax.dynamic_slice_in_dim(query, first, block, 0).astype(jnp.float32).reshape(block, KV_HEADS, group, HEAD)
        q_pos = first + jnp.arange(block, dtype=jnp.int32)
        q_seg = lax.dynamic_slice_in_dim(segment, first, block, 0)
        q_live = q_seg < DOCS - 1
        allowed = (segment[None, :] == q_seg[:, None]) & (positions[None, :] <= q_pos[:, None]) & q_live[:, None]

        def one_head(head_index):
            q_head = lax.dynamic_index_in_dim(q_blk, head_index, 1, keepdims=False)
            k_head = lax.dynamic_index_in_dim(keys_wide, head_index, 1, keepdims=False)
            v_head = lax.dynamic_index_in_dim(values_wide, head_index, 1, keepdims=False)
            scores = jnp.einsum('qgh,th->gqt', q_head, k_head) * scale
            scores = jnp.where(allowed[None], scores, neg_large)
            top = lax.optimization_barrier(jnp.max(scores, axis=2, keepdims=True))
            expo = jnp.where(allowed[None], jnp.exp(scores - top), 0.0)
            denom = lax.optimization_barrier(jnp.sum(expo, axis=2))
            weights = lax.optimization_barrier(expo.astype(jnp.bfloat16)).astype(jnp.float32)
            mixed = jnp.einsum('gqt,th->qgh', weights, v_head)
            return mixed / jnp.where(q_live[:, None], denom.T, 1.0)[:, :, None]
        outs = lax.map(one_head, jnp.arange(KV_HEADS, dtype=jnp.int32))
        outs = jnp.transpose(outs, (1, 0, 2, 3)).reshape(block, HEADS * HEAD)
        return jnp.where(q_live[:, None], outs, 0.0).astype(jnp.bfloat16)
    attended = lax.map(one_block, jnp.arange(stream // block, dtype=jnp.int32)).reshape(stream, HEADS * HEAD)
    pages = stream // PAGE
    stacked = jnp.stack([key.reshape(pages, PAGE, KV_HEADS * HEAD), value.reshape(pages, PAGE, KV_HEADS * HEAD)], axis=1)
    kv_cache = jnp.zeros_like(stacked).at[page_table].set(stacked)
    return (attended, kv_cache)

def math_sqrt(number):
    return float(number) ** 0.5
```

```python
import jax
import jax.numpy as jnp
from jax import lax
from jax.sharding import Mesh, PartitionSpec as P

D = 5120
HEADS = 40
KV_HEADS = 8
HEAD = 128
PAGE = 128


rope_base = 1000000.0
norm_eps = 1e-06
neg_large = -1e30


def token_meta(positions, lengths):
    ends = jnp.cumsum(lengths)
    past = (positions[:, None] >= ends[None, :]).astype(jnp.int32)
    segment = jnp.sum(past, axis=1)
    start = jnp.sum(past * lengths[None, :], axis=1)
    return (segment, positions - start)


def rotate(values, offsets):
    half = HEAD // 2
    freq = rope_base ** (-2.0 * jnp.arange(half, dtype=jnp.float32) / HEAD)
    angle = offsets.astype(jnp.float32)[:, None] * freq[None, :]
    cosine = jnp.cos(angle)[:, None, :]
    sine = jnp.sin(angle)[:, None, :]
    first = values[..., :half]
    second = values[..., half:]
    return jnp.concatenate(
        [first * cosine - second * sine, second * cosine + first * sine], axis=-1
    )


def on_device(
    tokens,
    norm_gain,
    w_query,
    w_key,
    w_value,
    query_bias,
    key_bias,
    value_bias,
    lengths,
    page_table,
):
    rows = tokens.shape[0]
    chips = lax.axis_size("chip")
    cores = lax.axis_size("core")
    blocks = chips * cores
    me = lax.axis_index("chip") * cores + lax.axis_index("core")
    q_width = w_query.shape[1]
    kv_width = w_key.shape[1]
    kv_dev = kv_width // HEAD
    group = HEADS // KV_HEADS
    slots = rows // PAGE
    docs = lengths.shape[0]
    scale = 1.0 / float(HEAD) ** 0.5
    wide = tokens.astype(jnp.float32)
    scaled = (wide * norm_gain.astype(jnp.float32)).astype(jnp.bfloat16)
    part_sq = jnp.sum(wide * wide, axis=1)
    width = tokens.shape[1]
    parts = lax.axis_size("tp")
    mine = lax.axis_index("tp")
    weights = (w_query, w_key, w_value)

    def project(chunk, source):
        return [
            jnp.dot(
                chunk,
                lax.dynamic_slice_in_dim(weight, source * width, width, 0),
                preferred_element_type=jnp.float32,
            )
            for weight in weights
        ]

    totals = project(scaled, mine)
    squares = part_sq
    for shift in range(1, parts):
        perm = [(j, (j + shift) % parts) for j in range(parts)]
        got = lax.ppermute(scaled, "tp", perm)
        got_sq = lax.ppermute(part_sq, "tp", perm)
        more = project(got, (mine + parts - shift) % parts)
        totals = [a + b for a, b in zip(totals, more)]
        squares = squares + got_sq
    proj_query, proj_key, proj_value = tuple(totals)
    rstd = lax.rsqrt(squares / D + norm_eps)
    own_pos = me * rows + jnp.arange(rows, dtype=jnp.int32)
    own_seg, own_off = token_meta(own_pos, lengths)
    own_live = own_seg < docs - 1
    query = rstd[:, None] * proj_query + query_bias.astype(jnp.float32)
    key = rstd[:, None] * proj_key + key_bias.astype(jnp.float32)
    value = rstd[:, None] * proj_value + value_bias.astype(jnp.float32)
    query = (
        rotate(query.reshape(rows, q_width // HEAD, HEAD), own_off)
        .reshape(rows, q_width)
        .astype(jnp.bfloat16)
    )
    key = (
        jnp.where(own_live[:, None, None], rotate(key.reshape(rows, kv_dev, HEAD), own_off), 0.0)
        .reshape(rows, kv_width)
        .astype(jnp.bfloat16)
    )
    value = jnp.where(own_live[:, None], value, 0.0).astype(jnp.bfloat16)
    q_seg, q_off = token_meta(own_pos, lengths)
    q_live = q_seg < docs - 1
    q_lo = jnp.min(jnp.where(q_live, own_pos - q_off, blocks * rows))
    q_hi = jnp.max(own_pos)
    q_grouped = query.reshape(rows, kv_dev, group, HEAD)

    def attend(state, key_block, value_block, key_start):
        best, total, acc = state
        count = key_block.shape[0]
        k_pos = key_start + jnp.arange(count, dtype=jnp.int32)
        k_seg, k_off = token_meta(k_pos, lengths)
        allowed = (
            (k_seg[None, :] == q_seg[:, None])
            & (k_pos[None, :] <= own_pos[:, None])
            & q_live[:, None]
        )
        scores = (
            jnp.einsum(
                "qcgh,tch->cgqt",
                q_grouped,
                key_block.reshape(count, kv_dev, HEAD),
                preferred_element_type=jnp.float32,
            )
            * scale
        )
        scores = jnp.where(allowed, scores, neg_large)
        fresh = jnp.maximum(best, jnp.max(scores, axis=3))
        expo = jnp.where(allowed, jnp.exp(scores - fresh[..., None]), 0.0)
        shrink = jnp.exp(best - fresh)
        total = total * shrink + jnp.sum(expo, axis=3)
        acc = acc * shrink[..., None] + jnp.einsum(
            "cgqt,tch->cgqh",
            expo.astype(jnp.bfloat16),
            value_block.reshape(count, kv_dev, HEAD),
            preferred_element_type=jnp.float32,
        )
        return (fresh, total, acc)

    start_state = (
        jnp.full((kv_dev, group, rows), neg_large, jnp.float32),
        jnp.zeros((kv_dev, group, rows), jnp.float32),
        jnp.zeros((kv_dev, group, rows, HEAD), jnp.float32),
    )
    start_state = start_state + (
        jnp.zeros((slots, PAGE * kv_width), jnp.float32),
        jnp.zeros((slots, PAGE * kv_width), jnp.float32),
    )
    both = jnp.concatenate([key, value], axis=1)
    both = lax.all_gather(both, "chip", axis=0, tiled=False)
    both = lax.all_gather(both, "core", axis=1, tiled=False)
    both = both.reshape(blocks * rows, 2 * kv_width)
    key_piece = both[:, :kv_width]
    value_piece = both[:, kv_width:]
    count = key_piece.shape[0]
    step = 512

    def one_step(index, state):
        first = index * step
        key_block = lax.dynamic_slice_in_dim(key_piece, first, step, 0)
        value_block = lax.dynamic_slice_in_dim(value_piece, first, step, 0)
        needed = (first <= q_hi) & (first + step - 1 >= q_lo)
        return lax.cond(
            needed,
            lambda held: attend(held, key_block, value_block, first),
            lambda held: held,
            state,
        )

    attention = lax.fori_loop(
        0, count // step, one_step, (start_state[0], start_state[1], start_state[2])
    )
    pages_here = count // PAGE
    pick = (page_table[None, :] == me * slots + jnp.arange(slots, dtype=jnp.int32)[:, None]).astype(
        jnp.bfloat16
    )
    cache_keys = jnp.dot(
        pick, key_piece.reshape(pages_here, PAGE * kv_width), preferred_element_type=jnp.float32
    )
    cache_values = jnp.dot(
        pick, value_piece.reshape(pages_here, PAGE * kv_width), preferred_element_type=jnp.float32
    )
    folded = attention + (cache_keys, cache_values)
    mixed = folded[2] / jnp.where(q_live, folded[1], 1.0)[..., None]
    mixed = jnp.transpose(mixed, (2, 0, 1, 3)).reshape(rows, q_width)
    mixed = jnp.where(q_live[:, None], mixed, 0.0).astype(jnp.bfloat16)
    kv_cache = (
        jnp.stack([folded[3], folded[4]], axis=1)
        .reshape(slots, 2, PAGE, kv_width)
        .astype(jnp.bfloat16)
    )
    return (mixed, kv_cache)


def solution(mesh):
    blocks = mesh.shape["blk"]
    split = Mesh(
        mesh.devices.reshape(blocks // 2, 2, mesh.shape["tp"]), ("chip", "core", "tp")
    )
    blk = ("chip", "core")
    in_specs = (
        P(blk, "tp"),
        P("tp"),
        P(None, "tp"),
        P(None, "tp"),
        P(None, "tp"),
        P("tp"),
        P("tp"),
        P("tp"),
        P(),
        P(),
    )
    out_specs = (P(blk, "tp"), P(blk, None, None, "tp"))
    return jax.shard_map(
        on_device, mesh=split, in_specs=in_specs, out_specs=out_specs, check_vma=False
    )
```

```python
import jax
import jax.numpy as jnp
from jax import lax
from jax.sharding import PartitionSpec as P

D = 5120
HEADS = 40
KV_HEADS = 8
HEAD = 128
PAGE = 128


rope_base = 1000000.0
norm_eps = 1e-06
neg_large = -1e30


def token_meta(positions, lengths):
    ends = jnp.cumsum(lengths)
    past = (positions[:, None] >= ends[None, :]).astype(jnp.int32)
    segment = jnp.sum(past, axis=1)
    start = jnp.sum(past * lengths[None, :], axis=1)
    return (segment, positions - start)


def rotate(values, offsets):
    half = HEAD // 2
    freq = rope_base ** (-2.0 * jnp.arange(half, dtype=jnp.float32) / HEAD)
    angle = offsets.astype(jnp.float32)[:, None] * freq[None, :]
    cosine = jnp.cos(angle)[:, None, :]
    sine = jnp.sin(angle)[:, None, :]
    first = values[..., :half]
    second = values[..., half:]
    return jnp.concatenate(
        [first * cosine - second * sine, second * cosine + first * sine], axis=-1
    )


def on_device(
    tokens,
    norm_gain,
    w_query,
    w_key,
    w_value,
    query_bias,
    key_bias,
    value_bias,
    lengths,
    page_table,
):
    rows = tokens.shape[0]
    blocks = lax.axis_size("blk")
    me = lax.axis_index("blk")
    q_width = w_query.shape[1]
    kv_width = w_key.shape[1]
    kv_dev = kv_width // HEAD
    group = HEADS // KV_HEADS
    slots = rows // PAGE
    docs = lengths.shape[0]
    scale = 1.0 / float(HEAD) ** 0.5
    wide = tokens.astype(jnp.float32)
    scaled = (wide * norm_gain.astype(jnp.float32)).astype(jnp.bfloat16)
    empty = (
        jnp.zeros((rows, q_width), jnp.float32),
        jnp.zeros((rows, kv_width), jnp.float32),
        jnp.zeros((rows, kv_width), jnp.float32),
    )
    piece = lax.all_gather(scaled, "tp", axis=1, tiled=True)
    count = piece.shape[1]
    totals = []
    for total, weight in zip(empty, (w_query, w_key, w_value)):
        totals.append(jnp.dot(piece, weight, preferred_element_type=jnp.float32))
    proj_query, proj_key, proj_value = tuple(totals)
    squares = lax.psum(jnp.sum(wide * wide, axis=1), "tp")
    rstd = lax.rsqrt(squares / D + norm_eps)
    own_pos = me * rows + jnp.arange(rows, dtype=jnp.int32)
    own_seg, own_off = token_meta(own_pos, lengths)
    own_live = own_seg < docs - 1
    query = rstd[:, None] * proj_query + query_bias.astype(jnp.float32)
    key = rstd[:, None] * proj_key + key_bias.astype(jnp.float32)
    value = rstd[:, None] * proj_value + value_bias.astype(jnp.float32)
    query = (
        rotate(query.reshape(rows, q_width // HEAD, HEAD), own_off)
        .reshape(rows, q_width)
        .astype(jnp.bfloat16)
    )
    key = (
        jnp.where(own_live[:, None, None], rotate(key.reshape(rows, kv_dev, HEAD), own_off), 0.0)
        .reshape(rows, kv_width)
        .astype(jnp.bfloat16)
    )
    value = jnp.where(own_live[:, None], value, 0.0).astype(jnp.bfloat16)
    q_seg, q_off = token_meta(own_pos, lengths)
    q_live = q_seg < docs - 1
    q_lo = jnp.min(jnp.where(q_live, own_pos - q_off, blocks * rows))
    q_hi = jnp.max(own_pos)
    q_grouped = query.reshape(rows, kv_dev, group, HEAD)

    def attend(state, key_block, value_block, key_start):
        best, total, acc = state
        count = key_block.shape[0]
        k_pos = key_start + jnp.arange(count, dtype=jnp.int32)
        k_seg, k_off = token_meta(k_pos, lengths)
        allowed = (
            (k_seg[None, :] == q_seg[:, None])
            & (k_pos[None, :] <= own_pos[:, None])
            & q_live[:, None]
        )
        scores = (
            jnp.einsum(
                "qcgh,tch->cgqt",
                q_grouped,
                key_block.reshape(count, kv_dev, HEAD),
                preferred_element_type=jnp.float32,
            )
            * scale
        )
        scores = jnp.where(allowed, scores, neg_large)
        fresh = jnp.maximum(best, jnp.max(scores, axis=3))
        expo = jnp.where(allowed, jnp.exp(scores - fresh[..., None]), 0.0)
        shrink = jnp.exp(best - fresh)
        total = total * shrink + jnp.sum(expo, axis=3)
        acc = acc * shrink[..., None] + jnp.einsum(
            "cgqt,tch->cgqh",
            expo.astype(jnp.bfloat16),
            value_block.reshape(count, kv_dev, HEAD),
            preferred_element_type=jnp.float32,
        )
        return (fresh, total, acc)

    start_state = (
        jnp.full((kv_dev, group, rows), neg_large, jnp.float32),
        jnp.zeros((kv_dev, group, rows), jnp.float32),
        jnp.zeros((kv_dev, group, rows, HEAD), jnp.float32),
    )
    both = lax.all_gather(jnp.concatenate([key, value], axis=1), "blk", axis=0, tiled=True)
    key_piece = both[:, :kv_width]
    value_piece = both[:, kv_width:]
    count = both.shape[0]
    step = rows

    def one_step(index, state):
        first = index * step
        key_block = lax.dynamic_slice_in_dim(key_piece, first, step, 0)
        value_block = lax.dynamic_slice_in_dim(value_piece, first, step, 0)
        needed = (first <= q_hi) & (first + step - 1 >= q_lo)
        return lax.cond(
            needed,
            lambda held: attend(held, key_block, value_block, first),
            lambda held: held,
            state,
        )

    attention = lax.fori_loop(
        0, count // step, one_step, (start_state[0], start_state[1], start_state[2])
    )
    numbers = jnp.arange(page_table.shape[0], dtype=jnp.int32)
    cache = []
    for j in range(slots):
        page = jnp.sum(jnp.where(page_table == me * slots + j, numbers, 0))
        held = lax.dynamic_slice_in_dim(both, page * PAGE, PAGE, 0)
        cache.append(jnp.stack([held[:, :kv_width], held[:, kv_width:]], axis=0))
    kv_cache = jnp.stack(cache, axis=0)
    mixed = attention[2] / jnp.where(q_live, attention[1], 1.0)[..., None]
    mixed = jnp.transpose(mixed, (2, 0, 1, 3)).reshape(rows, q_width)
    mixed = jnp.where(q_live[:, None], mixed, 0.0).astype(jnp.bfloat16)
    return (mixed, kv_cache)


def solution(mesh):
    in_specs = (
        P("blk", "tp"),
        P("tp"),
        P(None, "tp"),
        P(None, "tp"),
        P(None, "tp"),
        P("tp"),
        P("tp"),
        P("tp"),
        P(),
        P(),
    )
    out_specs = (P("blk", "tp"), P("blk", None, None, "tp"))
    return jax.shard_map(
        on_device, mesh=mesh, in_specs=in_specs, out_specs=out_specs, check_vma=False
    )
```

```python
import jax
import jax.numpy as jnp
from jax import lax
from jax.sharding import PartitionSpec as P

D = 5120
HEADS = 40
KV_HEADS = 8
HEAD = 128
PAGE = 128


rope_base = 1000000.0
norm_eps = 1e-06
neg_large = -1e30


def token_meta(positions, lengths):
    ends = jnp.cumsum(lengths)
    past = (positions[:, None] >= ends[None, :]).astype(jnp.int32)
    segment = jnp.sum(past, axis=1)
    start = jnp.sum(past * lengths[None, :], axis=1)
    return (segment, positions - start)


def rotate(values, offsets):
    half = HEAD // 2
    freq = rope_base ** (-2.0 * jnp.arange(half, dtype=jnp.float32) / HEAD)
    angle = offsets.astype(jnp.float32)[:, None] * freq[None, :]
    cosine = jnp.cos(angle)[:, None, :]
    sine = jnp.sin(angle)[:, None, :]
    first = values[..., :half]
    second = values[..., half:]
    return jnp.concatenate(
        [first * cosine - second * sine, second * cosine + first * sine], axis=-1
    )


def on_device(
    tokens,
    norm_gain,
    w_query,
    w_key,
    w_value,
    query_bias,
    key_bias,
    value_bias,
    lengths,
    page_table,
):
    rows = tokens.shape[0]
    blocks = lax.axis_size("blk")
    me = lax.axis_index("blk")
    q_width = w_query.shape[1]
    kv_width = w_key.shape[1]
    kv_dev = kv_width // HEAD
    group = HEADS // KV_HEADS
    slots = rows // PAGE
    docs = lengths.shape[0]
    scale = 1.0 / float(HEAD) ** 0.5
    wide = tokens.astype(jnp.float32)
    scaled = (wide * norm_gain.astype(jnp.float32)).astype(jnp.bfloat16)
    empty = (
        jnp.zeros((rows, q_width), jnp.float32),
        jnp.zeros((rows, kv_width), jnp.float32),
        jnp.zeros((rows, kv_width), jnp.float32),
    )
    piece = lax.all_gather(scaled, "tp", axis=1, tiled=True)
    count = piece.shape[1]
    totals = []
    for total, weight in zip(empty, (w_query, w_key, w_value)):
        totals.append(jnp.dot(piece, weight, preferred_element_type=jnp.float32))
    proj_query, proj_key, proj_value = tuple(totals)
    squares = lax.psum(jnp.sum(wide * wide, axis=1), "tp")
    rstd = lax.rsqrt(squares / D + norm_eps)
    own_pos = me * rows + jnp.arange(rows, dtype=jnp.int32)
    own_seg, own_off = token_meta(own_pos, lengths)
    own_live = own_seg < docs - 1
    query = rstd[:, None] * proj_query + query_bias.astype(jnp.float32)
    key = rstd[:, None] * proj_key + key_bias.astype(jnp.float32)
    value = rstd[:, None] * proj_value + value_bias.astype(jnp.float32)
    query = (
        rotate(query.reshape(rows, q_width // HEAD, HEAD), own_off)
        .reshape(rows, q_width)
        .astype(jnp.bfloat16)
    )
    key = (
        jnp.where(own_live[:, None, None], rotate(key.reshape(rows, kv_dev, HEAD), own_off), 0.0)
        .reshape(rows, kv_width)
        .astype(jnp.bfloat16)
    )
    value = jnp.where(own_live[:, None], value, 0.0).astype(jnp.bfloat16)
    q_seg, q_off = token_meta(own_pos, lengths)
    q_live = q_seg < docs - 1
    q_grouped = query.reshape(rows, kv_dev, group, HEAD)

    both = lax.all_gather(jnp.concatenate([key, value], axis=1), "blk", axis=0, tiled=True)
    count = both.shape[0]
    longest = count // 2
    span = min(count, longest + rows)
    first = jnp.clip(me * rows - longest, 0, count - span)
    window = lax.dynamic_slice_in_dim(both, first, span, 0)
    k_pos = first + jnp.arange(span, dtype=jnp.int32)
    k_seg, k_off = token_meta(k_pos, lengths)
    allowed = (
        (k_seg[None, :] == q_seg[:, None])
        & (k_pos[None, :] <= own_pos[:, None])
        & q_live[:, None]
    )
    scores = (
        jnp.einsum(
            "qcgh,tch->cgqt",
            q_grouped,
            window[:, :kv_width].reshape(span, kv_dev, HEAD),
            preferred_element_type=jnp.float32,
        )
        * scale
    )
    scores = jnp.where(allowed, scores, neg_large)
    top = jnp.max(scores, axis=3, keepdims=True)
    expo = jnp.where(allowed, jnp.exp(scores - top), 0.0)
    denom = jnp.sum(expo, axis=3)
    acc = jnp.einsum(
        "cgqt,tch->cgqh",
        expo.astype(jnp.bfloat16),
        window[:, kv_width:].reshape(span, kv_dev, HEAD),
        preferred_element_type=jnp.float32,
    )
    attention = (None, denom, acc)
    numbers = jnp.arange(page_table.shape[0], dtype=jnp.int32)
    cache = []
    for j in range(slots):
        page = jnp.sum(jnp.where(page_table == me * slots + j, numbers, 0))
        held = lax.dynamic_slice_in_dim(both, page * PAGE, PAGE, 0)
        cache.append(jnp.stack([held[:, :kv_width], held[:, kv_width:]], axis=0))
    kv_cache = jnp.stack(cache, axis=0)
    mixed = attention[2] / jnp.where(q_live, attention[1], 1.0)[..., None]
    mixed = jnp.transpose(mixed, (2, 0, 1, 3)).reshape(rows, q_width)
    mixed = jnp.where(q_live[:, None], mixed, 0.0).astype(jnp.bfloat16)
    return (mixed, kv_cache)


def solution(mesh):
    in_specs = (
        P("blk", "tp"),
        P("tp"),
        P(None, "tp"),
        P(None, "tp"),
        P(None, "tp"),
        P("tp"),
        P("tp"),
        P("tp"),
        P(),
        P(),
    )
    out_specs = (P("blk", "tp"), P("blk", None, None, "tp"))
    return jax.shard_map(
        on_device, mesh=mesh, in_specs=in_specs, out_specs=out_specs, check_vma=False
    )
```

```python
import jax
import jax.numpy as jnp
from jax import lax
from jax.experimental import pallas as pl
from jax.experimental.pallas import tpu as pltpu
from jax.sharding import PartitionSpec as P

D = 5120
HEADS = 40
KV_HEADS = 8
HEAD = 128
PAGE = 128


rope_base = 1000000.0
norm_eps = 1e-06
neg_large = -1e30


def token_meta(positions, lengths):
    ends = jnp.cumsum(lengths)
    past = (positions[:, None] >= ends[None, :]).astype(jnp.int32)
    segment = jnp.sum(past, axis=1)
    start = jnp.sum(past * lengths[None, :], axis=1)
    return (segment, positions - start)


def rotate(values, offsets):
    half = HEAD // 2
    freq = rope_base ** (-2.0 * jnp.arange(half, dtype=jnp.float32) / HEAD)
    angle = offsets.astype(jnp.float32)[:, None] * freq[None, :]
    cosine = jnp.cos(angle)[:, None, :]
    sine = jnp.sin(angle)[:, None, :]
    first = values[..., :half]
    second = values[..., half:]
    return jnp.concatenate(
        [first * cosine - second * sine, second * cosine + first * sine], axis=-1
    )


def window_attention(first, query, both, q_seg, q_pos, k_seg, k_pos, docs, interpret=False):
    rows, q_width = query.shape
    count, both_width = both.shape
    span = k_seg.shape[0]
    kv_dev = both_width // (2 * HEAD)
    group = q_width // (kv_dev * HEAD)
    scale = 1.0 / float(HEAD) ** 0.5

    def kernel(first_ref, q_ref, k_ref, v_ref, qs_ref, qp_ref, ks_ref, kp_ref, o_ref):
        start = pl.multiple_of(first_ref[0], PAGE)
        keys = k_ref[pl.ds(start, span), :]
        values = v_ref[pl.ds(start, span), :]
        qs = qs_ref[...]
        live = qs < docs - 1
        allowed = (ks_ref[...] == qs) & (kp_ref[...] <= qp_ref[...]) & live
        for g in range(group):
            q = q_ref[:, g * HEAD:(g + 1) * HEAD]
            scores = lax.dot_general(
                q, keys, (((1,), (1,)), ((), ())), preferred_element_type=jnp.float32
            ) * scale
            scores = jnp.where(allowed, scores, neg_large)
            top = jnp.max(scores, axis=1, keepdims=True)
            expo = jnp.where(allowed, jnp.exp(scores - top), 0.0)
            denom = jnp.sum(expo, axis=1, keepdims=True)
            acc = jnp.dot(expo.astype(jnp.bfloat16), values, preferred_element_type=jnp.float32)
            out = jnp.where(live, acc / jnp.where(live, denom, 1.0), 0.0)
            o_ref[:, g * HEAD:(g + 1) * HEAD] = out.astype(o_ref.dtype)

    spec = pltpu.PrefetchScalarGridSpec(
        num_scalar_prefetch=1,
        grid=(kv_dev,),
        in_specs=[
            pl.BlockSpec((rows, group * HEAD), lambda c, f: (0, c)),
            pl.BlockSpec((count, HEAD), lambda c, f: (0, c)),
            pl.BlockSpec((count, HEAD), lambda c, f: (0, kv_dev + c)),
            pl.BlockSpec((rows, 1), lambda c, f: (0, 0)),
            pl.BlockSpec((rows, 1), lambda c, f: (0, 0)),
            pl.BlockSpec((1, span), lambda c, f: (0, 0)),
            pl.BlockSpec((1, span), lambda c, f: (0, 0)),
        ],
        out_specs=pl.BlockSpec((rows, group * HEAD), lambda c, f: (0, c)),
    )
    return pl.pallas_call(
        kernel,
        grid_spec=spec,
        out_shape=jax.ShapeDtypeStruct((rows, q_width), jnp.bfloat16),
        interpret=interpret,
    )(
        first.reshape(1).astype(jnp.int32),
        query,
        both,
        both,
        q_seg.reshape(rows, 1),
        q_pos.reshape(rows, 1),
        k_seg.reshape(1, span),
        k_pos.reshape(1, span),
    )

def on_device(
    tokens,
    norm_gain,
    w_query,
    w_key,
    w_value,
    query_bias,
    key_bias,
    value_bias,
    lengths,
    page_table,
):
    rows = tokens.shape[0]
    blocks = lax.axis_size("blk")
    me = lax.axis_index("blk")
    q_width = w_query.shape[1]
    kv_width = w_key.shape[1]
    kv_dev = kv_width // HEAD
    group = HEADS // KV_HEADS
    slots = rows // PAGE
    docs = lengths.shape[0]
    scale = 1.0 / float(HEAD) ** 0.5
    wide = tokens.astype(jnp.float32)
    scaled = (wide * norm_gain.astype(jnp.float32)).astype(jnp.bfloat16)
    empty = (
        jnp.zeros((rows, q_width), jnp.float32),
        jnp.zeros((rows, kv_width), jnp.float32),
        jnp.zeros((rows, kv_width), jnp.float32),
    )
    piece = lax.all_gather(scaled, "tp", axis=1, tiled=True)
    count = piece.shape[1]
    totals = []
    for total, weight in zip(empty, (w_query, w_key, w_value)):
        totals.append(jnp.dot(piece, weight, preferred_element_type=jnp.float32))
    proj_query, proj_key, proj_value = tuple(totals)
    squares = lax.psum(jnp.sum(wide * wide, axis=1), "tp")
    rstd = lax.rsqrt(squares / D + norm_eps)
    own_pos = me * rows + jnp.arange(rows, dtype=jnp.int32)
    own_seg, own_off = token_meta(own_pos, lengths)
    own_live = own_seg < docs - 1
    query = rstd[:, None] * proj_query + query_bias.astype(jnp.float32)
    key = rstd[:, None] * proj_key + key_bias.astype(jnp.float32)
    value = rstd[:, None] * proj_value + value_bias.astype(jnp.float32)
    query = (
        rotate(query.reshape(rows, q_width // HEAD, HEAD), own_off)
        .reshape(rows, q_width)
        .astype(jnp.bfloat16)
    )
    key = (
        jnp.where(own_live[:, None, None], rotate(key.reshape(rows, kv_dev, HEAD), own_off), 0.0)
        .reshape(rows, kv_width)
        .astype(jnp.bfloat16)
    )
    value = jnp.where(own_live[:, None], value, 0.0).astype(jnp.bfloat16)
    q_seg, q_off = token_meta(own_pos, lengths)
    q_live = q_seg < docs - 1
    q_grouped = query.reshape(rows, kv_dev, group, HEAD)

    both = lax.all_gather(jnp.concatenate([key, value], axis=1), "blk", axis=0, tiled=True)
    count = both.shape[0]
    longest = count // 2
    span = min(count, longest + rows)
    first = jnp.clip(me * rows - longest, 0, count - span)
    k_pos = first + jnp.arange(span, dtype=jnp.int32)
    k_seg, k_off = token_meta(k_pos, lengths)
    mixed = window_attention(first, query, both, q_seg, own_pos, k_seg, k_pos, docs)
    numbers = jnp.arange(page_table.shape[0], dtype=jnp.int32)
    cache = []
    for j in range(slots):
        page = jnp.sum(jnp.where(page_table == me * slots + j, numbers, 0))
        held = lax.dynamic_slice_in_dim(both, page * PAGE, PAGE, 0)
        cache.append(jnp.stack([held[:, :kv_width], held[:, kv_width:]], axis=0))
    kv_cache = jnp.stack(cache, axis=0)
    return (mixed, kv_cache)


def solution(mesh):
    in_specs = (
        P("blk", "tp"),
        P("tp"),
        P(None, "tp"),
        P(None, "tp"),
        P(None, "tp"),
        P("tp"),
        P("tp"),
        P("tp"),
        P(),
        P(),
    )
    out_specs = (P("blk", "tp"), P("blk", None, None, "tp"))
    return jax.shard_map(
        on_device, mesh=mesh, in_specs=in_specs, out_specs=out_specs, check_vma=False
    )
```

```python
import jax
import jax.numpy as jnp
from jax import lax
from jax.experimental import pallas as pl
from jax.experimental.pallas import tpu as pltpu
from jax.sharding import PartitionSpec as P

D = 5120
HEADS = 40
KV_HEADS = 8
HEAD = 128
PAGE = 128


rope_base = 1000000.0
norm_eps = 1e-06
neg_large = -1e30


def token_meta(positions, lengths):
    ends = jnp.cumsum(lengths)
    past = (positions[:, None] >= ends[None, :]).astype(jnp.int32)
    segment = jnp.sum(past, axis=1)
    start = jnp.sum(past * lengths[None, :], axis=1)
    return (segment, positions - start)


def rotate(values, offsets):
    half = HEAD // 2
    freq = rope_base ** (-2.0 * jnp.arange(half, dtype=jnp.float32) / HEAD)
    angle = offsets.astype(jnp.float32)[:, None] * freq[None, :]
    cosine = jnp.cos(angle)[:, None, :]
    sine = jnp.sin(angle)[:, None, :]
    first = values[..., :half]
    second = values[..., half:]
    return jnp.concatenate(
        [first * cosine - second * sine, second * cosine + first * sine], axis=-1
    )


def window_attention(first, query, both, q_seg, q_pos, k_seg, k_pos, docs, interpret=False):
    rows, q_width = query.shape
    count, both_width = both.shape
    span = k_seg.shape[0]
    kv_dev = both_width // (2 * HEAD)
    group = q_width // (kv_dev * HEAD)
    scale = 1.0 / float(HEAD) ** 0.5

    def kernel(first_ref, q_ref, k_ref, v_ref, qs_ref, qp_ref, ks_ref, kp_ref, o_ref):
        start = pl.multiple_of(first_ref[0], PAGE)
        keys = k_ref[pl.ds(start, span), :]
        values = v_ref[pl.ds(start, span), :]
        qs = qs_ref[...]
        live = qs < docs - 1
        allowed = (ks_ref[...] == qs) & (kp_ref[...] <= qp_ref[...]) & live
        for g in range(group):
            q = q_ref[:, g * HEAD:(g + 1) * HEAD]
            scores = lax.dot_general(
                q, keys, (((1,), (1,)), ((), ())), preferred_element_type=jnp.float32
            ) * scale
            scores = jnp.where(allowed, scores, neg_large)
            top = jnp.max(scores, axis=1, keepdims=True)
            expo = jnp.where(allowed, jnp.exp(scores - top), 0.0)
            denom = jnp.sum(expo, axis=1, keepdims=True)
            acc = jnp.dot(expo.astype(jnp.bfloat16), values, preferred_element_type=jnp.float32)
            out = jnp.where(live, acc / jnp.where(live, denom, 1.0), 0.0)
            o_ref[:, g * HEAD:(g + 1) * HEAD] = out.astype(o_ref.dtype)

    spec = pltpu.PrefetchScalarGridSpec(
        num_scalar_prefetch=1,
        grid=(kv_dev,),
        in_specs=[
            pl.BlockSpec((rows, group * HEAD), lambda c, f: (0, c)),
            pl.BlockSpec((count, HEAD), lambda c, f: (0, c)),
            pl.BlockSpec((count, HEAD), lambda c, f: (0, kv_dev + c)),
            pl.BlockSpec((rows, 1), lambda c, f: (0, 0)),
            pl.BlockSpec((rows, 1), lambda c, f: (0, 0)),
            pl.BlockSpec((1, span), lambda c, f: (0, 0)),
            pl.BlockSpec((1, span), lambda c, f: (0, 0)),
        ],
        out_specs=pl.BlockSpec((rows, group * HEAD), lambda c, f: (0, c)),
    )
    return pl.pallas_call(
        kernel,
        grid_spec=spec,
        out_shape=jax.ShapeDtypeStruct((rows, q_width), jnp.bfloat16),
        interpret=interpret,
    )(
        first.reshape(1).astype(jnp.int32),
        query,
        both,
        both,
        q_seg.reshape(rows, 1),
        q_pos.reshape(rows, 1),
        k_seg.reshape(1, span),
        k_pos.reshape(1, span),
    )

def on_device(
    tokens,
    norm_gain,
    w_query,
    w_key,
    w_value,
    query_bias,
    key_bias,
    value_bias,
    lengths,
    page_table,
):
    rows = tokens.shape[0]
    blocks = lax.axis_size("blk")
    me = lax.axis_index("blk")
    q_width = w_query.shape[1]
    kv_width = w_key.shape[1]
    kv_dev = kv_width // HEAD
    group = HEADS // KV_HEADS
    slots = rows // PAGE
    docs = lengths.shape[0]
    scale = 1.0 / float(HEAD) ** 0.5
    wide = tokens.astype(jnp.float32)
    scaled = (wide * norm_gain.astype(jnp.float32)).astype(jnp.bfloat16)
    empty = (
        jnp.zeros((rows, q_width), jnp.float32),
        jnp.zeros((rows, kv_width), jnp.float32),
        jnp.zeros((rows, kv_width), jnp.float32),
    )
    part_sq = jnp.sum(wide * wide, axis=1)
    width = tokens.shape[1]
    parts = lax.axis_size("tp")
    mine = lax.axis_index("tp")
    weights = (w_query, w_key, w_value)
    half = rows // 2
    piece = lax.all_gather(scaled[:half], "tp", axis=1, tiled=True)
    upper = [jnp.dot(piece, weight, preferred_element_type=jnp.float32) for weight in weights]
    lower_rows = scaled[half:]

    def project(chunk, source):
        return [
            jnp.dot(
                chunk,
                lax.dynamic_slice_in_dim(weight, source * width, width, 0),
                preferred_element_type=jnp.float32,
            )
            for weight in weights
        ]

    lower = project(lower_rows, mine)
    squares = part_sq
    for shift in range(1, parts):
        perm = [(j, (j + shift) % parts) for j in range(parts)]
        got = lax.ppermute(lower_rows, "tp", perm)
        squares = squares + lax.ppermute(part_sq, "tp", perm)
        more = project(got, (mine + parts - shift) % parts)
        lower = [a + b for a, b in zip(lower, more)]
    proj_query, proj_key, proj_value = tuple(
        jnp.concatenate([a, b], axis=0) for a, b in zip(upper, lower)
    )
    rstd = lax.rsqrt(squares / D + norm_eps)
    own_pos = me * rows + jnp.arange(rows, dtype=jnp.int32)
    own_seg, own_off = token_meta(own_pos, lengths)
    own_live = own_seg < docs - 1
    query = rstd[:, None] * proj_query + query_bias.astype(jnp.float32)
    key = rstd[:, None] * proj_key + key_bias.astype(jnp.float32)
    value = rstd[:, None] * proj_value + value_bias.astype(jnp.float32)
    query = (
        rotate(query.reshape(rows, q_width // HEAD, HEAD), own_off)
        .reshape(rows, q_width)
        .astype(jnp.bfloat16)
    )
    key = (
        jnp.where(own_live[:, None, None], rotate(key.reshape(rows, kv_dev, HEAD), own_off), 0.0)
        .reshape(rows, kv_width)
        .astype(jnp.bfloat16)
    )
    value = jnp.where(own_live[:, None], value, 0.0).astype(jnp.bfloat16)
    q_seg, q_off = token_meta(own_pos, lengths)
    q_live = q_seg < docs - 1
    q_grouped = query.reshape(rows, kv_dev, group, HEAD)

    both = lax.all_gather(jnp.concatenate([key, value], axis=1), "blk", axis=0, tiled=True)
    count = both.shape[0]
    longest = count // 2
    span = min(count, longest + rows)
    first = jnp.clip(me * rows - longest, 0, count - span)
    k_pos = first + jnp.arange(span, dtype=jnp.int32)
    k_seg, k_off = token_meta(k_pos, lengths)
    mixed = window_attention(first, query, both, q_seg, own_pos, k_seg, k_pos, docs)
    numbers = jnp.arange(page_table.shape[0], dtype=jnp.int32)
    cache = []
    for j in range(slots):
        page = jnp.sum(jnp.where(page_table == me * slots + j, numbers, 0))
        held = lax.dynamic_slice_in_dim(both, page * PAGE, PAGE, 0)
        cache.append(jnp.stack([held[:, :kv_width], held[:, kv_width:]], axis=0))
    kv_cache = jnp.stack(cache, axis=0)
    return (mixed, kv_cache)


def solution(mesh):
    in_specs = (
        P("blk", "tp"),
        P("tp"),
        P(None, "tp"),
        P(None, "tp"),
        P(None, "tp"),
        P("tp"),
        P("tp"),
        P("tp"),
        P(),
        P(),
    )
    out_specs = (P("blk", "tp"), P("blk", None, None, "tp"))
    return jax.shard_map(
        on_device, mesh=mesh, in_specs=in_specs, out_specs=out_specs, check_vma=False
    )
```

```python
import jax
import jax.numpy as jnp
from jax import lax
from jax.experimental import pallas as pl
from jax.experimental.pallas import tpu as pltpu
from jax.sharding import PartitionSpec as P

D = 5120
HEADS = 40
KV_HEADS = 8
HEAD = 128
PAGE = 128


rope_base = 1000000.0
norm_eps = 1e-06
neg_large = -1e30


def token_meta(positions, lengths):
    ends = jnp.cumsum(lengths)
    past = (positions[:, None] >= ends[None, :]).astype(jnp.int32)
    segment = jnp.sum(past, axis=1)
    start = jnp.sum(past * lengths[None, :], axis=1)
    return (segment, positions - start)


def rotate(values, offsets):
    half = HEAD // 2
    freq = rope_base ** (-2.0 * jnp.arange(half, dtype=jnp.float32) / HEAD)
    angle = offsets.astype(jnp.float32)[:, None] * freq[None, :]
    cosine = jnp.cos(angle)[:, None, :]
    sine = jnp.sin(angle)[:, None, :]
    first = values[..., :half]
    second = values[..., half:]
    return jnp.concatenate(
        [first * cosine - second * sine, second * cosine + first * sine], axis=-1
    )


def window_attention(first, query, both, q_seg, q_pos, k_seg, k_pos, docs, interpret=False):
    rows, q_width = query.shape
    count, both_width = both.shape
    span = k_seg.shape[0]
    kv_dev = both_width // (2 * HEAD)
    group = q_width // (kv_dev * HEAD)
    scale = 1.0 / float(HEAD) ** 0.5

    def kernel(first_ref, q_ref, k_ref, v_ref, qs_ref, qp_ref, ks_ref, kp_ref, o_ref):
        start = pl.multiple_of(first_ref[0], PAGE)
        keys = k_ref[pl.ds(start, span), :]
        values = v_ref[pl.ds(start, span), :]
        qs = qs_ref[...]
        live = qs < docs - 1
        allowed = (ks_ref[...] == qs) & (kp_ref[...] <= qp_ref[...]) & live
        for g in range(group):
            q = q_ref[:, g * HEAD:(g + 1) * HEAD]
            scores = lax.dot_general(
                q, keys, (((1,), (1,)), ((), ())), preferred_element_type=jnp.float32
            ) * scale
            scores = jnp.where(allowed, scores, neg_large)
            top = jnp.max(scores, axis=1, keepdims=True)
            expo = jnp.where(allowed, jnp.exp(scores - top), 0.0)
            denom = jnp.sum(expo, axis=1, keepdims=True)
            acc = jnp.dot(expo.astype(jnp.bfloat16), values, preferred_element_type=jnp.float32)
            out = jnp.where(live, acc / jnp.where(live, denom, 1.0), 0.0)
            o_ref[:, g * HEAD:(g + 1) * HEAD] = out.astype(o_ref.dtype)

    spec = pltpu.PrefetchScalarGridSpec(
        num_scalar_prefetch=1,
        grid=(kv_dev,),
        in_specs=[
            pl.BlockSpec((rows, group * HEAD), lambda c, f: (0, c)),
            pl.BlockSpec((count, HEAD), lambda c, f: (0, c)),
            pl.BlockSpec((count, HEAD), lambda c, f: (0, kv_dev + c)),
            pl.BlockSpec((rows, 1), lambda c, f: (0, 0)),
            pl.BlockSpec((rows, 1), lambda c, f: (0, 0)),
            pl.BlockSpec((1, span), lambda c, f: (0, 0)),
            pl.BlockSpec((1, span), lambda c, f: (0, 0)),
        ],
        out_specs=pl.BlockSpec((rows, group * HEAD), lambda c, f: (0, c)),
    )
    return pl.pallas_call(
        kernel,
        grid_spec=spec,
        out_shape=jax.ShapeDtypeStruct((rows, q_width), jnp.bfloat16),
        interpret=interpret,
    )(
        first.reshape(1).astype(jnp.int32),
        query,
        both,
        both,
        q_seg.reshape(rows, 1),
        q_pos.reshape(rows, 1),
        k_seg.reshape(1, span),
        k_pos.reshape(1, span),
    )

def on_device(
    tokens,
    norm_gain,
    w_query,
    w_key,
    w_value,
    query_bias,
    key_bias,
    value_bias,
    lengths,
    page_table,
):
    rows = tokens.shape[0]
    blocks = lax.axis_size("blk")
    me = lax.axis_index("blk")
    q_width = w_query.shape[1]
    kv_width = w_key.shape[1]
    kv_dev = kv_width // HEAD
    group = HEADS // KV_HEADS
    slots = rows // PAGE
    docs = lengths.shape[0]
    scale = 1.0 / float(HEAD) ** 0.5
    wide = tokens.astype(jnp.float32)
    scaled = (wide * norm_gain.astype(jnp.float32)).astype(jnp.bfloat16)
    empty = (
        jnp.zeros((rows, q_width), jnp.float32),
        jnp.zeros((rows, kv_width), jnp.float32),
        jnp.zeros((rows, kv_width), jnp.float32),
    )
    part_sq = jnp.sum(wide * wide, axis=1)
    width = tokens.shape[1]
    parts = lax.axis_size("tp")
    mine = lax.axis_index("tp")
    weights = (w_query, w_key, w_value)
    half = rows // 2
    piece = lax.all_gather(scaled[:half], "tp", axis=1, tiled=True)
    upper = [jnp.dot(piece, weight, preferred_element_type=jnp.float32) for weight in weights]
    lower_rows = scaled[half:]

    def project(chunk, source):
        return [
            jnp.dot(
                chunk,
                lax.dynamic_slice_in_dim(weight, source * width, width, 0),
                preferred_element_type=jnp.float32,
            )
            for weight in weights
        ]

    lower = project(lower_rows, mine)
    squares = part_sq
    for shift in range(1, parts):
        perm = [(j, (j + shift) % parts) for j in range(parts)]
        got = lax.ppermute(lower_rows, "tp", perm)
        squares = squares + lax.ppermute(part_sq, "tp", perm)
        more = project(got, (mine + parts - shift) % parts)
        lower = [a + b for a, b in zip(lower, more)]
    rstd = lax.rsqrt(squares / D + norm_eps)
    own_pos = me * rows + jnp.arange(rows, dtype=jnp.int32)
    own_seg, own_off = token_meta(own_pos, lengths)
    own_live = own_seg < docs - 1

    def finish(totals, part):
        count_here = totals[0].shape[0]
        lo = part * half
        norm = rstd[lo:lo + count_here, None]
        off = own_off[lo:lo + count_here]
        live = own_live[lo:lo + count_here]
        query = norm * totals[0] + query_bias.astype(jnp.float32)
        key = norm * totals[1] + key_bias.astype(jnp.float32)
        value = norm * totals[2] + value_bias.astype(jnp.float32)
        query = (
            rotate(query.reshape(count_here, q_width // HEAD, HEAD), off)
            .reshape(count_here, q_width)
            .astype(jnp.bfloat16)
        )
        key = (
            jnp.where(live[:, None, None], rotate(key.reshape(count_here, kv_dev, HEAD), off), 0.0)
            .reshape(count_here, kv_width)
            .astype(jnp.bfloat16)
        )
        value = jnp.where(live[:, None], value, 0.0).astype(jnp.bfloat16)
        return query, jnp.concatenate([key, value], axis=1)

    query_up, kv_up = finish(upper, 0)
    query_low, kv_low = finish(lower, 1)
    query = jnp.concatenate([query_up, query_low], axis=0)
    key = jnp.concatenate([kv_up[:, :kv_width], kv_low[:, :kv_width]], axis=0)
    q_seg = own_seg
    q_live = own_live

    low_all = jnp.zeros((blocks,) + kv_low.shape, kv_low.dtype)
    low_all = lax.dynamic_update_slice_in_dim(low_all, kv_low[None], me, 0)
    for shift in range(1, blocks):
        perm = [(j, (j + shift) % blocks) for j in range(blocks)]
        got = lax.ppermute(kv_low, "blk", perm)
        low_all = lax.dynamic_update_slice_in_dim(
            low_all, got[None], (me + blocks - shift) % blocks, 0
        )
    up_all = lax.all_gather(kv_up, "blk", axis=0, tiled=False)
    both = jnp.stack([up_all, low_all], axis=1).reshape(blocks * rows, 2 * kv_width)
    count = both.shape[0]
    longest = count // 2
    span = min(count, longest + rows)
    first = jnp.clip(me * rows - longest, 0, count - span)
    k_pos = first + jnp.arange(span, dtype=jnp.int32)
    k_seg, k_off = token_meta(k_pos, lengths)
    mixed = window_attention(first, query, both, q_seg, own_pos, k_seg, k_pos, docs)
    numbers = jnp.arange(page_table.shape[0], dtype=jnp.int32)
    cache = []
    for j in range(slots):
        page = jnp.sum(jnp.where(page_table == me * slots + j, numbers, 0))
        held = lax.dynamic_slice_in_dim(both, page * PAGE, PAGE, 0)
        cache.append(jnp.stack([held[:, :kv_width], held[:, kv_width:]], axis=0))
    kv_cache = jnp.stack(cache, axis=0)
    return (mixed, kv_cache)


def solution(mesh):
    in_specs = (
        P("blk", "tp"),
        P("tp"),
        P(None, "tp"),
        P(None, "tp"),
        P(None, "tp"),
        P("tp"),
        P("tp"),
        P("tp"),
        P(),
        P(),
    )
    out_specs = (P("blk", "tp"), P("blk", None, None, "tp"))
    return jax.shard_map(
        on_device, mesh=mesh, in_specs=in_specs, out_specs=out_specs, check_vma=False
    )
```

```python
import jax
import jax.numpy as jnp
from jax import lax
from jax.experimental import pallas as pl
from jax.experimental.pallas import tpu as pltpu
from jax.sharding import PartitionSpec as P

D = 5120
HEADS = 40
KV_HEADS = 8
HEAD = 128
PAGE = 128


rope_base = 1000000.0
norm_eps = 1e-06
neg_large = -1e30


def token_meta(positions, lengths):
    ends = jnp.cumsum(lengths)
    past = (positions[:, None] >= ends[None, :]).astype(jnp.int32)
    segment = jnp.sum(past, axis=1)
    start = jnp.sum(past * lengths[None, :], axis=1)
    return (segment, positions - start)


def rotate(values, offsets):
    half = HEAD // 2
    freq = rope_base ** (-2.0 * jnp.arange(half, dtype=jnp.float32) / HEAD)
    angle = offsets.astype(jnp.float32)[:, None] * freq[None, :]
    cosine = jnp.cos(angle)[:, None, :]
    sine = jnp.sin(angle)[:, None, :]
    first = values[..., :half]
    second = values[..., half:]
    return jnp.concatenate(
        [first * cosine - second * sine, second * cosine + first * sine], axis=-1
    )


def window_attention(first, query, both, q_seg, q_pos, k_seg, k_pos, docs, interpret=False):
    rows, q_width = query.shape
    count, both_width = both.shape
    span = k_seg.shape[0]
    kv_dev = both_width // (2 * HEAD)
    group = q_width // (kv_dev * HEAD)
    scale = 1.0 / float(HEAD) ** 0.5

    def kernel(first_ref, q_ref, k_ref, v_ref, qs_ref, qp_ref, ks_ref, kp_ref, o_ref):
        start = pl.multiple_of(first_ref[0], PAGE)
        keys = k_ref[pl.ds(start, span), :]
        values = v_ref[pl.ds(start, span), :]
        qs = qs_ref[...]
        live = qs < docs - 1
        allowed = (ks_ref[...] == qs) & (kp_ref[...] <= qp_ref[...]) & live
        for g in range(group):
            q = q_ref[:, g * HEAD:(g + 1) * HEAD]
            scores = lax.dot_general(
                q, keys, (((1,), (1,)), ((), ())), preferred_element_type=jnp.float32
            ) * scale
            scores = jnp.where(allowed, scores, neg_large)
            top = jnp.max(scores, axis=1, keepdims=True)
            expo = jnp.exp(scores - top)
            denom = jnp.sum(expo, axis=1, keepdims=True)
            acc = jnp.dot(expo.astype(jnp.bfloat16), values, preferred_element_type=jnp.float32)
            out = jnp.where(live, acc / jnp.where(live, denom, 1.0), 0.0)
            o_ref[:, g * HEAD:(g + 1) * HEAD] = out.astype(o_ref.dtype)

    spec = pltpu.PrefetchScalarGridSpec(
        num_scalar_prefetch=1,
        grid=(kv_dev,),
        in_specs=[
            pl.BlockSpec((rows, group * HEAD), lambda c, f: (0, c)),
            pl.BlockSpec((count, HEAD), lambda c, f: (0, c)),
            pl.BlockSpec((count, HEAD), lambda c, f: (0, kv_dev + c)),
            pl.BlockSpec((rows, 1), lambda c, f: (0, 0)),
            pl.BlockSpec((rows, 1), lambda c, f: (0, 0)),
            pl.BlockSpec((1, span), lambda c, f: (0, 0)),
            pl.BlockSpec((1, span), lambda c, f: (0, 0)),
        ],
        out_specs=pl.BlockSpec((rows, group * HEAD), lambda c, f: (0, c)),
    )
    return pl.pallas_call(
        kernel,
        grid_spec=spec,
        out_shape=jax.ShapeDtypeStruct((rows, q_width), jnp.bfloat16),
        interpret=interpret,
    )(
        first.reshape(1).astype(jnp.int32),
        query,
        both,
        both,
        q_seg.reshape(rows, 1),
        q_pos.reshape(rows, 1),
        k_seg.reshape(1, span),
        k_pos.reshape(1, span),
    )

def on_device(
    tokens,
    norm_gain,
    w_query,
    w_key,
    w_value,
    query_bias,
    key_bias,
    value_bias,
    lengths,
    page_table,
):
    rows = tokens.shape[0]
    blocks = lax.axis_size("blk")
    me = lax.axis_index("blk")
    q_width = w_query.shape[1]
    kv_width = w_key.shape[1]
    kv_dev = kv_width // HEAD
    group = HEADS // KV_HEADS
    slots = rows // PAGE
    docs = lengths.shape[0]
    scale = 1.0 / float(HEAD) ** 0.5
    wide = tokens.astype(jnp.float32)
    scaled = (wide * norm_gain.astype(jnp.float32)).astype(jnp.bfloat16)
    part_sq = jnp.sum(wide * wide, axis=1)
    parts = lax.axis_size("tp")
    squares = part_sq
    for shift in range(1, parts):
        perm = [(j, (j + shift) % parts) for j in range(parts)]
        squares = squares + lax.ppermute(part_sq, "tp", perm)
    piece = lax.all_gather(scaled, "tp", axis=1, tiled=True)
    w_kv = jnp.concatenate([w_key, w_value], axis=1)
    proj_kv = jnp.dot(piece, w_kv, preferred_element_type=jnp.float32)
    proj_query = jnp.dot(piece, w_query, preferred_element_type=jnp.float32)
    proj_key = proj_kv[:, :kv_width]
    proj_value = proj_kv[:, kv_width:]
    rstd = lax.rsqrt(squares / D + norm_eps)
    own_pos = me * rows + jnp.arange(rows, dtype=jnp.int32)
    own_seg, own_off = token_meta(own_pos, lengths)
    own_live = own_seg < docs - 1
    query = rstd[:, None] * proj_query + query_bias.astype(jnp.float32)
    key = rstd[:, None] * proj_key + key_bias.astype(jnp.float32)
    value = rstd[:, None] * proj_value + value_bias.astype(jnp.float32)
    query = (
        rotate(query.reshape(rows, q_width // HEAD, HEAD), own_off)
        .reshape(rows, q_width)
        .astype(jnp.bfloat16)
    )
    key = (
        jnp.where(own_live[:, None, None], rotate(key.reshape(rows, kv_dev, HEAD), own_off), 0.0)
        .reshape(rows, kv_width)
        .astype(jnp.bfloat16)
    )
    value = jnp.where(own_live[:, None], value, 0.0).astype(jnp.bfloat16)
    q_seg, q_off = token_meta(own_pos, lengths)
    q_live = q_seg < docs - 1
    q_grouped = query.reshape(rows, kv_dev, group, HEAD)

    both = lax.all_gather(jnp.concatenate([key, value], axis=1), "blk", axis=0, tiled=True)
    count = both.shape[0]
    longest = count // 2
    span = min(count, longest + rows)
    first = jnp.clip(me * rows - longest, 0, count - span)
    k_pos = first + jnp.arange(span, dtype=jnp.int32)
    k_seg, k_off = token_meta(k_pos, lengths)
    mixed = window_attention(first, query, both, q_seg, own_pos, k_seg, k_pos, docs)
    numbers = jnp.arange(page_table.shape[0], dtype=jnp.int32)
    cache = []
    for j in range(slots):
        page = jnp.sum(jnp.where(page_table == me * slots + j, numbers, 0))
        held = lax.dynamic_slice_in_dim(both, page * PAGE, PAGE, 0)
        cache.append(jnp.stack([held[:, :kv_width], held[:, kv_width:]], axis=0))
    kv_cache = jnp.stack(cache, axis=0)
    return (mixed, kv_cache)


def solution(mesh):
    in_specs = (
        P("blk", "tp"),
        P("tp"),
        P(None, "tp"),
        P(None, "tp"),
        P(None, "tp"),
        P("tp"),
        P("tp"),
        P("tp"),
        P(),
        P(),
    )
    out_specs = (P("blk", "tp"), P("blk", None, None, "tp"))
    return jax.shard_map(
        on_device, mesh=mesh, in_specs=in_specs, out_specs=out_specs, check_vma=False
    )
```

```python
import jax
import jax.numpy as jnp
from jax import lax
from jax.experimental import pallas as pl
from jax.experimental.pallas import tpu as pltpu
from jax.sharding import PartitionSpec as P

D = 5120
HEADS = 40
KV_HEADS = 8
HEAD = 128
PAGE = 128


rope_base = 1000000.0
norm_eps = 1e-06
neg_large = -1e30


def token_meta(positions, lengths):
    ends = jnp.cumsum(lengths)
    past = (positions[:, None] >= ends[None, :]).astype(jnp.int32)
    segment = jnp.sum(past, axis=1)
    start = jnp.sum(past * lengths[None, :], axis=1)
    return (segment, positions - start)


def rotate(values, offsets):
    half = HEAD // 2
    freq = rope_base ** (-2.0 * jnp.arange(half, dtype=jnp.float32) / HEAD)
    angle = offsets.astype(jnp.float32)[:, None] * freq[None, :]
    cosine = jnp.cos(angle)[:, None, :]
    sine = jnp.sin(angle)[:, None, :]
    first = values[..., :half]
    second = values[..., half:]
    return jnp.concatenate(
        [first * cosine - second * sine, second * cosine + first * sine], axis=-1
    )


def partners(size):
    if size & (size - 1) == 0:
        return [
            ((lambda i, s=s: jnp.bitwise_xor(i, s)), [(j, j ^ s) for j in range(size)])
            for s in range(1, size)
        ]
    return [
        ((lambda i, s=s: (i + size - s) % size), [(j, (j + s) % size) for j in range(size)])
        for s in range(1, size)
    ]

def window_attention(first, query, both, q_seg, q_pos, k_seg, k_pos, docs, interpret=False):
    rows, q_width = query.shape
    count, both_width = both.shape
    span = k_seg.shape[0]
    kv_dev = both_width // (2 * HEAD)
    group = q_width // (kv_dev * HEAD)
    scale = 1.0 / float(HEAD) ** 0.5

    def kernel(first_ref, q_ref, k_ref, v_ref, qs_ref, qp_ref, ks_ref, kp_ref, o_ref):
        start = pl.multiple_of(first_ref[0], PAGE)
        keys = k_ref[pl.ds(start, span), :]
        values = v_ref[pl.ds(start, span), :]
        qs = qs_ref[...]
        live = qs < docs - 1
        allowed = (ks_ref[...] == qs) & (kp_ref[...] <= qp_ref[...]) & live
        for g in range(group):
            q = q_ref[:, g * HEAD:(g + 1) * HEAD]
            scores = lax.dot_general(
                q, keys, (((1,), (1,)), ((), ())), preferred_element_type=jnp.float32
            ) * scale
            scores = jnp.where(allowed, scores, neg_large)
            top = jnp.max(scores, axis=1, keepdims=True)
            expo = jnp.exp(scores - top)
            denom = jnp.sum(expo, axis=1, keepdims=True)
            acc = jnp.dot(expo.astype(jnp.bfloat16), values, preferred_element_type=jnp.float32)
            out = jnp.where(live, acc / jnp.where(live, denom, 1.0), 0.0)
            o_ref[:, g * HEAD:(g + 1) * HEAD] = out.astype(o_ref.dtype)

    spec = pltpu.PrefetchScalarGridSpec(
        num_scalar_prefetch=1,
        grid=(kv_dev,),
        in_specs=[
            pl.BlockSpec((rows, group * HEAD), lambda c, f: (0, c)),
            pl.BlockSpec((count, HEAD), lambda c, f: (0, c)),
            pl.BlockSpec((count, HEAD), lambda c, f: (0, kv_dev + c)),
            pl.BlockSpec((rows, 1), lambda c, f: (0, 0)),
            pl.BlockSpec((rows, 1), lambda c, f: (0, 0)),
            pl.BlockSpec((1, span), lambda c, f: (0, 0)),
            pl.BlockSpec((1, span), lambda c, f: (0, 0)),
        ],
        out_specs=pl.BlockSpec((rows, group * HEAD), lambda c, f: (0, c)),
    )
    return pl.pallas_call(
        kernel,
        grid_spec=spec,
        out_shape=jax.ShapeDtypeStruct((rows, q_width), jnp.bfloat16),
        interpret=interpret,
    )(
        first.reshape(1).astype(jnp.int32),
        query,
        both,
        both,
        q_seg.reshape(rows, 1),
        q_pos.reshape(rows, 1),
        k_seg.reshape(1, span),
        k_pos.reshape(1, span),
    )

def on_device(
    tokens,
    norm_gain,
    w_query,
    w_key,
    w_value,
    query_bias,
    key_bias,
    value_bias,
    lengths,
    page_table,
):
    rows = tokens.shape[0]
    blocks = lax.axis_size("blk")
    me = lax.axis_index("blk")
    q_width = w_query.shape[1]
    kv_width = w_key.shape[1]
    kv_dev = kv_width // HEAD
    group = HEADS // KV_HEADS
    slots = rows // PAGE
    docs = lengths.shape[0]
    scale = 1.0 / float(HEAD) ** 0.5
    wide = tokens.astype(jnp.float32)
    scaled = (wide * norm_gain.astype(jnp.float32)).astype(jnp.bfloat16)
    part_sq = jnp.sum(wide * wide, axis=1)
    parts = lax.axis_size("tp")
    squares = part_sq
    for flip, perm in partners(parts):
        squares = squares + lax.ppermute(part_sq, "tp", perm)
    w_kv = jnp.concatenate([w_key, w_value], axis=1)
    width = tokens.shape[1]
    mine = lax.axis_index("tp")

    def project(chunk, source):
        return [
            jnp.dot(
                chunk,
                lax.dynamic_slice_in_dim(weight, source * width, width, 0),
                preferred_element_type=jnp.float32,
            )
            for weight in (w_kv, w_query)
        ]

    proj_kv, proj_query = project(scaled, mine)
    for flip, perm in partners(parts):
        got = lax.ppermute(scaled, "tp", perm)
        more = project(got, flip(mine))
        proj_kv = proj_kv + more[0]
        proj_query = proj_query + more[1]
    proj_key = proj_kv[:, :kv_width]
    proj_value = proj_kv[:, kv_width:]
    rstd = lax.rsqrt(squares / D + norm_eps)
    own_pos = me * rows + jnp.arange(rows, dtype=jnp.int32)
    own_seg, own_off = token_meta(own_pos, lengths)
    own_live = own_seg < docs - 1
    query = rstd[:, None] * proj_query + query_bias.astype(jnp.float32)
    key = rstd[:, None] * proj_key + key_bias.astype(jnp.float32)
    value = rstd[:, None] * proj_value + value_bias.astype(jnp.float32)
    query = (
        rotate(query.reshape(rows, q_width // HEAD, HEAD), own_off)
        .reshape(rows, q_width)
        .astype(jnp.bfloat16)
    )
    key = (
        jnp.where(own_live[:, None, None], rotate(key.reshape(rows, kv_dev, HEAD), own_off), 0.0)
        .reshape(rows, kv_width)
        .astype(jnp.bfloat16)
    )
    value = jnp.where(own_live[:, None], value, 0.0).astype(jnp.bfloat16)
    q_seg, q_off = token_meta(own_pos, lengths)
    q_live = q_seg < docs - 1
    q_grouped = query.reshape(rows, kv_dev, group, HEAD)

    own_kv = jnp.concatenate([key, value], axis=1)
    both = jnp.zeros((blocks,) + own_kv.shape, own_kv.dtype)
    both = lax.dynamic_update_slice_in_dim(both, own_kv[None], me, 0)
    for flip, perm in partners(blocks):
        got = lax.ppermute(own_kv, "blk", perm)
        both = lax.dynamic_update_slice_in_dim(both, got[None], flip(me), 0)
    both = both.reshape(blocks * rows, 2 * kv_width)
    count = both.shape[0]
    longest = count // 2
    span = min(count, longest + rows)
    first = jnp.clip(me * rows - longest, 0, count - span)
    k_pos = first + jnp.arange(span, dtype=jnp.int32)
    k_seg, k_off = token_meta(k_pos, lengths)
    mixed = window_attention(first, query, both, q_seg, own_pos, k_seg, k_pos, docs)
    numbers = jnp.arange(page_table.shape[0], dtype=jnp.int32)
    cache = []
    for j in range(slots):
        page = jnp.sum(jnp.where(page_table == me * slots + j, numbers, 0))
        held = lax.dynamic_slice_in_dim(both, page * PAGE, PAGE, 0)
        cache.append(jnp.stack([held[:, :kv_width], held[:, kv_width:]], axis=0))
    kv_cache = jnp.stack(cache, axis=0)
    return (mixed, kv_cache)


def solution(mesh):
    in_specs = (
        P("blk", "tp"),
        P("tp"),
        P(None, "tp"),
        P(None, "tp"),
        P(None, "tp"),
        P("tp"),
        P("tp"),
        P("tp"),
        P(),
        P(),
    )
    out_specs = (P("blk", "tp"), P("blk", None, None, "tp"))
    return jax.shard_map(
        on_device, mesh=mesh, in_specs=in_specs, out_specs=out_specs, check_vma=False
    )
```

```python
import jax
import jax.numpy as jnp
from jax import lax
from jax.experimental import pallas as pl
from jax.experimental.pallas import tpu as pltpu
from jax.sharding import PartitionSpec as P

D = 5120
HEADS = 40
KV_HEADS = 8
HEAD = 128
PAGE = 128


rope_base = 1000000.0
norm_eps = 1e-06
neg_large = -1e30


def token_meta(positions, lengths):
    ends = jnp.cumsum(lengths)
    past = (positions[:, None] >= ends[None, :]).astype(jnp.int32)
    segment = jnp.sum(past, axis=1)
    start = jnp.sum(past * lengths[None, :], axis=1)
    return (segment, positions - start)


def rotate(values, offsets):
    half = HEAD // 2
    freq = rope_base ** (-2.0 * jnp.arange(half, dtype=jnp.float32) / HEAD)
    angle = offsets.astype(jnp.float32)[:, None] * freq[None, :]
    cosine = jnp.cos(angle)[:, None, :]
    sine = jnp.sin(angle)[:, None, :]
    first = values[..., :half]
    second = values[..., half:]
    return jnp.concatenate(
        [first * cosine - second * sine, second * cosine + first * sine], axis=-1
    )


def partners(size):
    if size & (size - 1) == 0:
        return [
            ((lambda i, s=s: jnp.bitwise_xor(i, s)), [(j, j ^ s) for j in range(size)])
            for s in range(1, size)
        ]
    return [
        ((lambda i, s=s: (i + size - s) % size), [(j, (j + s) % size) for j in range(size)])
        for s in range(1, size)
    ]

def window_attention(first, query, both, q_seg, q_pos, k_seg, k_pos, docs, interpret=False):
    rows, q_width = query.shape
    count, both_width = both.shape
    span = k_seg.shape[0]
    kv_dev = both_width // (2 * HEAD)
    group = q_width // (kv_dev * HEAD)
    scale = 1.0 / float(HEAD) ** 0.5

    def kernel(first_ref, q_ref, k_ref, v_ref, qs_ref, qp_ref, ks_ref, kp_ref, o_ref):
        start = pl.multiple_of(first_ref[0], PAGE)
        keys = k_ref[pl.ds(start, span), :]
        values = v_ref[pl.ds(start, span), :]
        qs = qs_ref[...]
        live = qs < docs - 1
        allowed = (ks_ref[...] == qs) & (kp_ref[...] <= qp_ref[...]) & live
        for g in range(group):
            q = q_ref[:, g * HEAD:(g + 1) * HEAD]
            scores = lax.dot_general(
                q, keys, (((1,), (1,)), ((), ())), preferred_element_type=jnp.float32
            ) * scale
            scores = jnp.where(allowed, scores, neg_large)
            top = jnp.max(scores, axis=1, keepdims=True)
            expo = jnp.exp(scores - top)
            denom = jnp.sum(expo, axis=1, keepdims=True)
            acc = jnp.dot(expo.astype(jnp.bfloat16), values, preferred_element_type=jnp.float32)
            out = jnp.where(live, acc / jnp.where(live, denom, 1.0), 0.0)
            o_ref[:, g * HEAD:(g + 1) * HEAD] = out.astype(o_ref.dtype)

    spec = pltpu.PrefetchScalarGridSpec(
        num_scalar_prefetch=1,
        grid=(kv_dev,),
        in_specs=[
            pl.BlockSpec((rows, group * HEAD), lambda c, f: (0, c)),
            pl.BlockSpec((count, HEAD), lambda c, f: (0, c)),
            pl.BlockSpec((count, HEAD), lambda c, f: (0, kv_dev + c)),
            pl.BlockSpec((rows, 1), lambda c, f: (0, 0)),
            pl.BlockSpec((rows, 1), lambda c, f: (0, 0)),
            pl.BlockSpec((1, span), lambda c, f: (0, 0)),
            pl.BlockSpec((1, span), lambda c, f: (0, 0)),
        ],
        out_specs=pl.BlockSpec((rows, group * HEAD), lambda c, f: (0, c)),
    )
    return pl.pallas_call(
        kernel,
        grid_spec=spec,
        out_shape=jax.ShapeDtypeStruct((rows, q_width), jnp.bfloat16),
        interpret=interpret,
    )(
        first.reshape(1).astype(jnp.int32),
        query,
        both,
        both,
        q_seg.reshape(rows, 1),
        q_pos.reshape(rows, 1),
        k_seg.reshape(1, span),
        k_pos.reshape(1, span),
    )

def on_device(
    tokens,
    norm_gain,
    w_query,
    w_key,
    w_value,
    query_bias,
    key_bias,
    value_bias,
    lengths,
    page_table,
):
    rows = tokens.shape[0]
    blocks = lax.axis_size("blk")
    me = lax.axis_index("blk")
    q_width = w_query.shape[1]
    kv_width = w_key.shape[1]
    kv_dev = kv_width // HEAD
    group = HEADS // KV_HEADS
    slots = rows // PAGE
    docs = lengths.shape[0]
    scale = 1.0 / float(HEAD) ** 0.5
    wide = tokens.astype(jnp.float32)
    scaled = (wide * norm_gain.astype(jnp.float32)).astype(jnp.bfloat16)
    part_sq = jnp.sum(wide * wide, axis=1)
    parts = lax.axis_size("tp")
    squares = part_sq
    for flip, perm in partners(parts):
        squares = squares + lax.ppermute(part_sq, "tp", perm)
    w_kv = jnp.concatenate([w_key, w_value], axis=1)
    width = tokens.shape[1]
    mine = lax.axis_index("tp")

    def project(chunk, source):
        return [
            jnp.dot(
                chunk,
                lax.dynamic_slice_in_dim(weight, source * width, width, 0),
                preferred_element_type=jnp.float32,
            )
            for weight in (w_kv, w_query)
        ]

    proj_kv, proj_query = project(scaled, mine)
    for flip, perm in partners(parts):
        got = lax.ppermute(scaled, "tp", perm)
        more = project(got, flip(mine))
        proj_kv = proj_kv + more[0]
        proj_query = proj_query + more[1]
    proj_key = proj_kv[:, :kv_width]
    proj_value = proj_kv[:, kv_width:]
    rstd = lax.rsqrt(squares / D + norm_eps)
    own_pos = me * rows + jnp.arange(rows, dtype=jnp.int32)
    own_seg, own_off = token_meta(own_pos, lengths)
    own_live = own_seg < docs - 1
    query = rstd[:, None] * proj_query + query_bias.astype(jnp.float32)
    key = rstd[:, None] * proj_key + key_bias.astype(jnp.float32)
    value = rstd[:, None] * proj_value + value_bias.astype(jnp.float32)
    query = (
        rotate(query.reshape(rows, q_width // HEAD, HEAD), own_off)
        .reshape(rows, q_width)
        .astype(jnp.bfloat16)
    )
    key = (
        jnp.where(own_live[:, None, None], rotate(key.reshape(rows, kv_dev, HEAD), own_off), 0.0)
        .reshape(rows, kv_width)
        .astype(jnp.bfloat16)
    )
    value = jnp.where(own_live[:, None], value, 0.0).astype(jnp.bfloat16)
    q_seg, q_off = token_meta(own_pos, lengths)
    q_live = q_seg < docs - 1
    q_grouped = query.reshape(rows, kv_dev, group, HEAD)

    both = lax.all_gather(jnp.concatenate([key, value], axis=1), "blk", axis=0, tiled=True)
    count = both.shape[0]
    longest = count // 2
    span = min(count, longest + rows)
    first = jnp.clip(me * rows - longest, 0, count - span)
    k_pos = first + jnp.arange(span, dtype=jnp.int32)
    k_seg, k_off = token_meta(k_pos, lengths)
    mixed = window_attention(first, query, both, q_seg, own_pos, k_seg, k_pos, docs)
    numbers = jnp.arange(page_table.shape[0], dtype=jnp.int32)
    cache = []
    for j in range(slots):
        page = jnp.sum(jnp.where(page_table == me * slots + j, numbers, 0))
        held = lax.dynamic_slice_in_dim(both, page * PAGE, PAGE, 0)
        cache.append(jnp.stack([held[:, :kv_width], held[:, kv_width:]], axis=0))
    kv_cache = jnp.stack(cache, axis=0)
    return (mixed, kv_cache)


def solution(mesh):
    in_specs = (
        P("blk", "tp"),
        P("tp"),
        P(None, "tp"),
        P(None, "tp"),
        P(None, "tp"),
        P("tp"),
        P("tp"),
        P("tp"),
        P(),
        P(),
    )
    out_specs = (P("blk", "tp"), P("blk", None, None, "tp"))
    return jax.shard_map(
        on_device, mesh=mesh, in_specs=in_specs, out_specs=out_specs, check_vma=False
    )
```

```python
import jax
import jax.numpy as jnp
from jax import lax
from jax.experimental import pallas as pl
from jax.experimental.pallas import tpu as pltpu
from jax.sharding import PartitionSpec as P

D = 5120
HEADS = 40
KV_HEADS = 8
HEAD = 128
PAGE = 128


rope_base = 1000000.0
norm_eps = 1e-06
neg_large = -1e30


def token_meta(positions, lengths):
    ends = jnp.cumsum(lengths)
    past = (positions[:, None] >= ends[None, :]).astype(jnp.int32)
    segment = jnp.sum(past, axis=1)
    start = jnp.sum(past * lengths[None, :], axis=1)
    return (segment, positions - start)


def rotate(values, offsets):
    half = HEAD // 2
    freq = rope_base ** (-2.0 * jnp.arange(half, dtype=jnp.float32) / HEAD)
    angle = offsets.astype(jnp.float32)[:, None] * freq[None, :]
    cosine = jnp.cos(angle)[:, None, :]
    sine = jnp.sin(angle)[:, None, :]
    first = values[..., :half]
    second = values[..., half:]
    return jnp.concatenate(
        [first * cosine - second * sine, second * cosine + first * sine], axis=-1
    )


def partners(size):
    if size & (size - 1) == 0:
        return [
            ((lambda i, s=s: jnp.bitwise_xor(i, s)), [(j, j ^ s) for j in range(size)])
            for s in range(1, size)
        ]
    return [
        ((lambda i, s=s: (i + size - s) % size), [(j, (j + s) % size) for j in range(size)])
        for s in range(1, size)
    ]

def window_attention(first, query, both, q_seg, q_pos, k_seg, k_pos, docs, interpret=False):
    rows, q_width = query.shape
    count, both_width = both.shape
    span = k_seg.shape[0]
    kv_dev = both_width // (2 * HEAD)
    group = q_width // (kv_dev * HEAD)
    scale = 1.0 / float(HEAD) ** 0.5

    def kernel(first_ref, q_ref, k_ref, v_ref, qs_ref, qp_ref, ks_ref, kp_ref, o_ref):
        start = pl.multiple_of(first_ref[0], PAGE)
        keys = k_ref[pl.ds(start, span), :]
        values = v_ref[pl.ds(start, span), :]
        qs = qs_ref[...]
        live = qs < docs - 1
        allowed = (ks_ref[...] == qs) & (kp_ref[...] <= qp_ref[...]) & live
        for g in range(group):
            q = q_ref[:, g * HEAD:(g + 1) * HEAD]
            scores = lax.dot_general(
                q, keys, (((1,), (1,)), ((), ())), preferred_element_type=jnp.float32
            ) * scale
            scores = jnp.where(allowed, scores, neg_large)
            top = jnp.max(scores, axis=1, keepdims=True)
            expo = jnp.exp(scores - top)
            denom = jnp.sum(expo, axis=1, keepdims=True)
            acc = jnp.dot(expo.astype(jnp.bfloat16), values, preferred_element_type=jnp.float32)
            out = jnp.where(live, acc / jnp.where(live, denom, 1.0), 0.0)
            o_ref[:, g * HEAD:(g + 1) * HEAD] = out.astype(o_ref.dtype)

    spec = pltpu.PrefetchScalarGridSpec(
        num_scalar_prefetch=1,
        grid=(kv_dev,),
        in_specs=[
            pl.BlockSpec((rows, group * HEAD), lambda c, f: (0, c)),
            pl.BlockSpec((count, HEAD), lambda c, f: (0, c)),
            pl.BlockSpec((count, HEAD), lambda c, f: (0, kv_dev + c)),
            pl.BlockSpec((rows, 1), lambda c, f: (0, 0)),
            pl.BlockSpec((rows, 1), lambda c, f: (0, 0)),
            pl.BlockSpec((1, span), lambda c, f: (0, 0)),
            pl.BlockSpec((1, span), lambda c, f: (0, 0)),
        ],
        out_specs=pl.BlockSpec((rows, group * HEAD), lambda c, f: (0, c)),
    )
    return pl.pallas_call(
        kernel,
        grid_spec=spec,
        out_shape=jax.ShapeDtypeStruct((rows, q_width), jnp.bfloat16),
        interpret=interpret,
    )(
        first.reshape(1).astype(jnp.int32),
        query,
        both,
        both,
        q_seg.reshape(rows, 1),
        q_pos.reshape(rows, 1),
        k_seg.reshape(1, span),
        k_pos.reshape(1, span),
    )

def on_device(
    tokens,
    norm_gain,
    w_query,
    w_key,
    w_value,
    query_bias,
    key_bias,
    value_bias,
    lengths,
    page_table,
):
    rows = tokens.shape[0]
    blocks = lax.axis_size("blk")
    me = lax.axis_index("blk")
    q_width = w_query.shape[1]
    kv_width = w_key.shape[1]
    kv_dev = kv_width // HEAD
    group = HEADS // KV_HEADS
    slots = rows // PAGE
    docs = lengths.shape[0]
    scale = 1.0 / float(HEAD) ** 0.5
    wide = tokens.astype(jnp.float32)
    scaled = (wide * norm_gain.astype(jnp.float32)).astype(jnp.bfloat16)
    part_sq = jnp.sum(wide * wide, axis=1)
    parts = lax.axis_size("tp")
    squares = part_sq
    for flip, perm in partners(parts):
        squares = squares + lax.ppermute(part_sq, "tp", perm)
    w_kv = jnp.concatenate([w_key, w_value], axis=1)
    width = tokens.shape[1]
    mine = lax.axis_index("tp")

    def project(chunk, source):
        return [
            jnp.dot(
                chunk,
                lax.dynamic_slice_in_dim(weight, source * width, width, 0),
                preferred_element_type=jnp.float32,
            )
            for weight in (w_kv, w_query)
        ]

    proj_kv, proj_query = project(scaled, mine)
    for flip, perm in partners(parts):
        got = lax.ppermute(scaled, "tp", perm)
        more = project(got, flip(mine))
        proj_kv = proj_kv + more[0]
        proj_query = proj_query + more[1]
    proj_key = proj_kv[:, :kv_width]
    proj_value = proj_kv[:, kv_width:]
    rstd = lax.rsqrt(squares / D + norm_eps)
    own_pos = me * rows + jnp.arange(rows, dtype=jnp.int32)
    own_seg, own_off = token_meta(own_pos, lengths)
    own_live = own_seg < docs - 1
    query = rstd[:, None] * proj_query + query_bias.astype(jnp.float32)
    key = rstd[:, None] * proj_key + key_bias.astype(jnp.float32)
    value = rstd[:, None] * proj_value + value_bias.astype(jnp.float32)
    query = (
        rotate(query.reshape(rows, q_width // HEAD, HEAD), own_off)
        .reshape(rows, q_width)
        .astype(jnp.bfloat16)
    )
    key = (
        jnp.where(own_live[:, None, None], rotate(key.reshape(rows, kv_dev, HEAD), own_off), 0.0)
        .reshape(rows, kv_width)
        .astype(jnp.bfloat16)
    )
    value = jnp.where(own_live[:, None], value, 0.0).astype(jnp.bfloat16)
    q_seg, q_off = token_meta(own_pos, lengths)
    q_live = q_seg < docs - 1
    q_grouped = query.reshape(rows, kv_dev, group, HEAD)

    own_kv = jnp.concatenate([key, value], axis=1)
    chips = blocks // 2
    chip = me // 2
    core = me % 2
    rightward = [(i, i + 2) for i in range(blocks - 2)]
    leftward = [(i, i - 2) for i in range(2, blocks)]
    near = [own_kv] * (2 * chips - 1)
    from_left = own_kv
    from_right = own_kv
    for step in range(1, chips):
        from_left = lax.ppermute(from_left, "blk", rightward)
        from_right = lax.ppermute(from_right, "blk", leftward)
        near[chips - 1 - step] = from_left
        near[chips - 1 + step] = from_right
    same_core = lax.dynamic_slice_in_dim(jnp.stack(near, axis=0), chips - 1 - chip, chips, 0)
    other_core = lax.ppermute(same_core, "blk", [(i, i ^ 1) for i in range(blocks)])
    both = jnp.stack(
        [
            jnp.where(core == 0, same_core, other_core),
            jnp.where(core == 0, other_core, same_core),
        ],
        axis=1,
    ).reshape(blocks * rows, 2 * kv_width)
    count = both.shape[0]
    longest = count // 2
    span = min(count, longest + rows)
    first = jnp.clip(me * rows - longest, 0, count - span)
    k_pos = first + jnp.arange(span, dtype=jnp.int32)
    k_seg, k_off = token_meta(k_pos, lengths)
    mixed = window_attention(first, query, both, q_seg, own_pos, k_seg, k_pos, docs)
    numbers = jnp.arange(page_table.shape[0], dtype=jnp.int32)
    cache = []
    for j in range(slots):
        page = jnp.sum(jnp.where(page_table == me * slots + j, numbers, 0))
        held = lax.dynamic_slice_in_dim(both, page * PAGE, PAGE, 0)
        cache.append(jnp.stack([held[:, :kv_width], held[:, kv_width:]], axis=0))
    kv_cache = jnp.stack(cache, axis=0)
    return (mixed, kv_cache)


def solution(mesh):
    in_specs = (
        P("blk", "tp"),
        P("tp"),
        P(None, "tp"),
        P(None, "tp"),
        P(None, "tp"),
        P("tp"),
        P("tp"),
        P("tp"),
        P(),
        P(),
    )
    out_specs = (P("blk", "tp"), P("blk", None, None, "tp"))
    return jax.shard_map(
        on_device, mesh=mesh, in_specs=in_specs, out_specs=out_specs, check_vma=False
    )
```

```python
import jax
import jax.numpy as jnp
from jax import lax
from jax.experimental import pallas as pl
from jax.experimental.pallas import tpu as pltpu
from jax.sharding import PartitionSpec as P

D = 5120
HEADS = 40
KV_HEADS = 8
HEAD = 128
PAGE = 128


rope_base = 1000000.0
norm_eps = 1e-06
neg_large = -1e30


def token_meta(positions, lengths):
    ends = jnp.cumsum(lengths)
    past = (positions[:, None] >= ends[None, :]).astype(jnp.int32)
    segment = jnp.sum(past, axis=1)
    start = jnp.sum(past * lengths[None, :], axis=1)
    return (segment, positions - start)


def rotate(values, offsets):
    half = HEAD // 2
    freq = rope_base ** (-2.0 * jnp.arange(half, dtype=jnp.float32) / HEAD)
    angle = offsets.astype(jnp.float32)[:, None] * freq[None, :]
    cosine = jnp.cos(angle)[:, None, :]
    sine = jnp.sin(angle)[:, None, :]
    first = values[..., :half]
    second = values[..., half:]
    return jnp.concatenate(
        [first * cosine - second * sine, second * cosine + first * sine], axis=-1
    )


def partners(size):
    if size & (size - 1) == 0:
        return [
            ((lambda i, s=s: jnp.bitwise_xor(i, s)), [(j, j ^ s) for j in range(size)])
            for s in range(1, size)
        ]
    return [
        ((lambda i, s=s: (i + size - s) % size), [(j, (j + s) % size) for j in range(size)])
        for s in range(1, size)
    ]

def window_attention(first, query, both, q_seg, q_pos, k_seg, k_pos, docs, interpret=False):
    rows, q_width = query.shape
    count, both_width = both.shape
    span = k_seg.shape[0]
    kv_dev = both_width // (2 * HEAD)
    group = q_width // (kv_dev * HEAD)
    scale = 1.0 / float(HEAD) ** 0.5

    def kernel(first_ref, q_ref, k_ref, v_ref, qs_ref, qp_ref, ks_ref, kp_ref, o_ref):
        start = pl.multiple_of(first_ref[0], PAGE)
        keys = k_ref[pl.ds(start, span), :]
        values = v_ref[pl.ds(start, span), :]
        qs = qs_ref[...]
        live = qs < docs - 1
        allowed = (ks_ref[...] == qs) & (kp_ref[...] <= qp_ref[...]) & live
        for g in range(group):
            q = q_ref[:, g * HEAD:(g + 1) * HEAD]
            scores = lax.dot_general(
                q, keys, (((1,), (1,)), ((), ())), preferred_element_type=jnp.float32
            ) * scale
            scores = jnp.where(allowed, scores, neg_large)
            top = jnp.max(scores, axis=1, keepdims=True)
            expo = jnp.exp(scores - top)
            denom = jnp.sum(expo, axis=1, keepdims=True)
            acc = jnp.dot(expo.astype(jnp.bfloat16), values, preferred_element_type=jnp.float32)
            out = jnp.where(live, acc / jnp.where(live, denom, 1.0), 0.0)
            o_ref[:, g * HEAD:(g + 1) * HEAD] = out.astype(o_ref.dtype)

    spec = pltpu.PrefetchScalarGridSpec(
        num_scalar_prefetch=1,
        grid=(kv_dev,),
        in_specs=[
            pl.BlockSpec((rows, group * HEAD), lambda c, f: (0, c)),
            pl.BlockSpec((count, HEAD), lambda c, f: (0, c)),
            pl.BlockSpec((count, HEAD), lambda c, f: (0, kv_dev + c)),
            pl.BlockSpec((rows, 1), lambda c, f: (0, 0)),
            pl.BlockSpec((rows, 1), lambda c, f: (0, 0)),
            pl.BlockSpec((1, span), lambda c, f: (0, 0)),
            pl.BlockSpec((1, span), lambda c, f: (0, 0)),
        ],
        out_specs=pl.BlockSpec((rows, group * HEAD), lambda c, f: (0, c)),
    )
    return pl.pallas_call(
        kernel,
        grid_spec=spec,
        out_shape=jax.ShapeDtypeStruct((rows, q_width), jnp.bfloat16),
        interpret=interpret,
    )(
        first.reshape(1).astype(jnp.int32),
        query,
        both,
        both,
        q_seg.reshape(rows, 1),
        q_pos.reshape(rows, 1),
        k_seg.reshape(1, span),
        k_pos.reshape(1, span),
    )

def on_device(
    tokens,
    norm_gain,
    w_query,
    w_key,
    w_value,
    query_bias,
    key_bias,
    value_bias,
    lengths,
    page_table,
):
    rows = tokens.shape[0]
    blocks = lax.axis_size("blk")
    me = lax.axis_index("blk")
    q_width = w_query.shape[1]
    kv_width = w_key.shape[1]
    kv_dev = kv_width // HEAD
    group = HEADS // KV_HEADS
    slots = rows // PAGE
    docs = lengths.shape[0]
    scale = 1.0 / float(HEAD) ** 0.5
    wide = tokens.astype(jnp.float32)
    scaled = (wide * norm_gain.astype(jnp.float32)).astype(jnp.bfloat16)
    part_sq = jnp.sum(wide * wide, axis=1)
    parts = lax.axis_size("tp")
    squares = part_sq
    w_kv = jnp.concatenate([w_key, w_value], axis=1)
    width = tokens.shape[1]
    mine = lax.axis_index("tp")

    def project(chunk, source):
        return [
            jnp.dot(
                chunk,
                lax.dynamic_slice_in_dim(weight, source * width, width, 0),
                preferred_element_type=jnp.float32,
            )
            for weight in (w_kv, w_query)
        ]

    proj_kv, proj_query = project(scaled, mine)
    extended = jnp.concatenate(
        [tokens, norm_gain[None, :], jnp.zeros((15, width), tokens.dtype)], axis=0
    )
    for flip, perm in partners(parts):
        got = lax.ppermute(extended, "tp", perm)
        got_wide = got[:rows].astype(jnp.float32)
        squares = squares + jnp.sum(got_wide * got_wide, axis=1)
        got_scaled = (got_wide * got[rows].astype(jnp.float32)[None, :]).astype(jnp.bfloat16)
        more = project(got_scaled, flip(mine))
        proj_kv = proj_kv + more[0]
        proj_query = proj_query + more[1]
    proj_key = proj_kv[:, :kv_width]
    proj_value = proj_kv[:, kv_width:]
    rstd = lax.rsqrt(squares / D + norm_eps)
    own_pos = me * rows + jnp.arange(rows, dtype=jnp.int32)
    own_seg, own_off = token_meta(own_pos, lengths)
    own_live = own_seg < docs - 1
    query = rstd[:, None] * proj_query + query_bias.astype(jnp.float32)
    key = rstd[:, None] * proj_key + key_bias.astype(jnp.float32)
    value = rstd[:, None] * proj_value + value_bias.astype(jnp.float32)
    query = (
        rotate(query.reshape(rows, q_width // HEAD, HEAD), own_off)
        .reshape(rows, q_width)
        .astype(jnp.bfloat16)
    )
    key = (
        jnp.where(own_live[:, None, None], rotate(key.reshape(rows, kv_dev, HEAD), own_off), 0.0)
        .reshape(rows, kv_width)
        .astype(jnp.bfloat16)
    )
    value = jnp.where(own_live[:, None], value, 0.0).astype(jnp.bfloat16)
    q_seg, q_off = token_meta(own_pos, lengths)
    q_live = q_seg < docs - 1
    q_grouped = query.reshape(rows, kv_dev, group, HEAD)

    both = lax.all_gather(jnp.concatenate([key, value], axis=1), "blk", axis=0, tiled=True)
    count = both.shape[0]
    longest = count // 2
    span = min(count, longest + rows)
    first = jnp.clip(me * rows - longest, 0, count - span)
    k_pos = first + jnp.arange(span, dtype=jnp.int32)
    k_seg, k_off = token_meta(k_pos, lengths)
    mixed = window_attention(first, query, both, q_seg, own_pos, k_seg, k_pos, docs)
    numbers = jnp.arange(page_table.shape[0], dtype=jnp.int32)
    cache = []
    for j in range(slots):
        page = jnp.sum(jnp.where(page_table == me * slots + j, numbers, 0))
        held = lax.dynamic_slice_in_dim(both, page * PAGE, PAGE, 0)
        cache.append(jnp.stack([held[:, :kv_width], held[:, kv_width:]], axis=0))
    kv_cache = jnp.stack(cache, axis=0)
    return (mixed, kv_cache)


def solution(mesh):
    in_specs = (
        P("blk", "tp"),
        P("tp"),
        P(None, "tp"),
        P(None, "tp"),
        P(None, "tp"),
        P("tp"),
        P("tp"),
        P("tp"),
        P(),
        P(),
    )
    out_specs = (P("blk", "tp"), P("blk", None, None, "tp"))
    return jax.shard_map(
        on_device, mesh=mesh, in_specs=in_specs, out_specs=out_specs, check_vma=False
    )
```

```python
import jax
import jax.numpy as jnp
from jax import lax
from jax.experimental import pallas as pl
from jax.experimental.pallas import tpu as pltpu
from jax.sharding import PartitionSpec as P

D = 5120
HEADS = 40
KV_HEADS = 8
HEAD = 128
PAGE = 128


rope_base = 1000000.0
norm_eps = 1e-06
neg_large = -1e30


def token_meta(positions, lengths):
    ends = jnp.cumsum(lengths)
    past = (positions[:, None] >= ends[None, :]).astype(jnp.int32)
    segment = jnp.sum(past, axis=1)
    start = jnp.sum(past * lengths[None, :], axis=1)
    return (segment, positions - start)


def rotate(values, offsets):
    half = HEAD // 2
    freq = rope_base ** (-2.0 * jnp.arange(half, dtype=jnp.float32) / HEAD)
    angle = offsets.astype(jnp.float32)[:, None] * freq[None, :]
    cosine = jnp.cos(angle)[:, None, :]
    sine = jnp.sin(angle)[:, None, :]
    first = values[..., :half]
    second = values[..., half:]
    return jnp.concatenate(
        [first * cosine - second * sine, second * cosine + first * sine], axis=-1
    )


def partners(size):
    if size & (size - 1) == 0:
        return [
            ((lambda i, s=s: jnp.bitwise_xor(i, s)), [(j, j ^ s) for j in range(size)])
            for s in range(1, size)
        ]
    return [
        ((lambda i, s=s: (i + size - s) % size), [(j, (j + s) % size) for j in range(size)])
        for s in range(1, size)
    ]

def window_attention(first, query, both, q_seg, q_pos, k_seg, k_pos, docs, interpret=False):
    rows, q_width = query.shape
    count, both_width = both.shape
    span = k_seg.shape[0]
    kv_dev = both_width // (2 * HEAD)
    group = q_width // (kv_dev * HEAD)
    scale = 1.0 / float(HEAD) ** 0.5

    def kernel(first_ref, q_ref, k_ref, v_ref, qs_ref, qp_ref, ks_ref, kp_ref, o_ref):
        start = pl.multiple_of(first_ref[0], PAGE)
        keys = k_ref[pl.ds(start, span), :]
        values = v_ref[pl.ds(start, span), :]
        qs = qs_ref[...]
        live = qs < docs - 1
        allowed = (ks_ref[...] == qs) & (kp_ref[...] <= qp_ref[...]) & live
        for g in range(group):
            q = q_ref[:, g * HEAD:(g + 1) * HEAD]
            scores = lax.dot_general(
                q, keys, (((1,), (1,)), ((), ())), preferred_element_type=jnp.float32
            ) * scale
            scores = jnp.where(allowed, scores, neg_large)
            top = jnp.max(scores, axis=1, keepdims=True)
            expo = jnp.exp(scores - top)
            denom = jnp.sum(expo, axis=1, keepdims=True)
            acc = jnp.dot(expo.astype(jnp.bfloat16), values, preferred_element_type=jnp.float32)
            out = jnp.where(live, acc / jnp.where(live, denom, 1.0), 0.0)
            o_ref[:, g * HEAD:(g + 1) * HEAD] = out.astype(o_ref.dtype)

    spec = pltpu.PrefetchScalarGridSpec(
        num_scalar_prefetch=1,
        grid=(kv_dev,),
        in_specs=[
            pl.BlockSpec((rows, group * HEAD), lambda c, f: (0, c)),
            pl.BlockSpec((count, HEAD), lambda c, f: (0, c)),
            pl.BlockSpec((count, HEAD), lambda c, f: (0, kv_dev + c)),
            pl.BlockSpec((rows, 1), lambda c, f: (0, 0)),
            pl.BlockSpec((rows, 1), lambda c, f: (0, 0)),
            pl.BlockSpec((1, span), lambda c, f: (0, 0)),
            pl.BlockSpec((1, span), lambda c, f: (0, 0)),
        ],
        out_specs=pl.BlockSpec((rows, group * HEAD), lambda c, f: (0, c)),
    )
    return pl.pallas_call(
        kernel,
        grid_spec=spec,
        out_shape=jax.ShapeDtypeStruct((rows, q_width), jnp.bfloat16),
        interpret=interpret,
    )(
        first.reshape(1).astype(jnp.int32),
        query,
        both,
        both,
        q_seg.reshape(rows, 1),
        q_pos.reshape(rows, 1),
        k_seg.reshape(1, span),
        k_pos.reshape(1, span),
    )

def on_device(
    tokens,
    norm_gain,
    w_query,
    w_key,
    w_value,
    query_bias,
    key_bias,
    value_bias,
    lengths,
    page_table,
):
    rows = tokens.shape[0]
    blocks = lax.axis_size("blk")
    me = lax.axis_index("blk")
    q_width = w_query.shape[1]
    kv_width = w_key.shape[1]
    kv_dev = kv_width // HEAD
    group = HEADS // KV_HEADS
    slots = rows // PAGE
    docs = lengths.shape[0]
    scale = 1.0 / float(HEAD) ** 0.5
    wide = tokens.astype(jnp.float32)
    scaled = (wide * norm_gain.astype(jnp.float32)).astype(jnp.bfloat16)
    part_sq = jnp.sum(wide * wide, axis=1)
    parts = lax.axis_size("tp")
    squares = part_sq
    for flip, perm in partners(parts):
        squares = squares + lax.ppermute(part_sq, "tp", perm)
    w_kv = jnp.concatenate([w_key, w_value], axis=1)
    width = tokens.shape[1]
    mine = lax.axis_index("tp")

    def project(chunk, source):
        return [
            jnp.dot(
                chunk,
                lax.dynamic_slice_in_dim(weight, source * width, width, 0),
                preferred_element_type=jnp.float32,
            )
            for weight in (w_kv, w_query)
        ]

    rstd = lax.rsqrt(squares / D + norm_eps)
    own_pos = me * rows + jnp.arange(rows, dtype=jnp.int32)
    own_seg, own_off = token_meta(own_pos, lengths)
    own_live = own_seg < docs - 1
    q_seg = own_seg
    q_live = own_live
    half = rows // 2

    def finish(lo):
        chunk = scaled[lo:lo + half]
        proj_kv, proj_query = project(chunk, mine)
        for flip, perm in partners(parts):
            got = lax.ppermute(chunk, "tp", perm)
            more = project(got, flip(mine))
            proj_kv = proj_kv + more[0]
            proj_query = proj_query + more[1]
        norm = rstd[lo:lo + half, None]
        off = own_off[lo:lo + half]
        live = own_live[lo:lo + half]
        query = norm * proj_query + query_bias.astype(jnp.float32)
        key = norm * proj_kv[:, :kv_width] + key_bias.astype(jnp.float32)
        value = norm * proj_kv[:, kv_width:] + value_bias.astype(jnp.float32)
        query = (
            rotate(query.reshape(half, q_width // HEAD, HEAD), off)
            .reshape(half, q_width)
            .astype(jnp.bfloat16)
        )
        key = (
            jnp.where(live[:, None, None], rotate(key.reshape(half, kv_dev, HEAD), off), 0.0)
            .reshape(half, kv_width)
            .astype(jnp.bfloat16)
        )
        value = jnp.where(live[:, None], value, 0.0).astype(jnp.bfloat16)
        gathered = lax.all_gather(jnp.concatenate([key, value], axis=1), "blk", axis=0, tiled=False)
        return query, gathered

    query_up, kv_up = finish(0)
    query_low, kv_low = finish(half)
    query = jnp.concatenate([query_up, query_low], axis=0)
    both = jnp.stack([kv_up, kv_low], axis=1).reshape(blocks * rows, 2 * kv_width)
    count = both.shape[0]
    longest = count // 2
    span = min(count, longest + rows)
    first = jnp.clip(me * rows - longest, 0, count - span)
    k_pos = first + jnp.arange(span, dtype=jnp.int32)
    k_seg, k_off = token_meta(k_pos, lengths)
    mixed = window_attention(first, query, both, q_seg, own_pos, k_seg, k_pos, docs)
    numbers = jnp.arange(page_table.shape[0], dtype=jnp.int32)
    cache = []
    for j in range(slots):
        page = jnp.sum(jnp.where(page_table == me * slots + j, numbers, 0))
        held = lax.dynamic_slice_in_dim(both, page * PAGE, PAGE, 0)
        cache.append(jnp.stack([held[:, :kv_width], held[:, kv_width:]], axis=0))
    kv_cache = jnp.stack(cache, axis=0)
    return (mixed, kv_cache)


def solution(mesh):
    in_specs = (
        P("blk", "tp"),
        P("tp"),
        P(None, "tp"),
        P(None, "tp"),
        P(None, "tp"),
        P("tp"),
        P("tp"),
        P("tp"),
        P(),
        P(),
    )
    out_specs = (P("blk", "tp"), P("blk", None, None, "tp"))
    return jax.shard_map(
        on_device, mesh=mesh, in_specs=in_specs, out_specs=out_specs, check_vma=False
    )
```

```python
import jax
import jax.numpy as jnp
from jax import lax
from jax.experimental import pallas as pl
from jax.experimental.pallas import tpu as pltpu
from jax.sharding import PartitionSpec as P

D = 5120
HEADS = 40
KV_HEADS = 8
HEAD = 128
PAGE = 128


rope_base = 1000000.0
norm_eps = 1e-06
neg_large = -1e30


def token_meta(positions, lengths):
    ends = jnp.cumsum(lengths)
    past = (positions[:, None] >= ends[None, :]).astype(jnp.int32)
    segment = jnp.sum(past, axis=1)
    start = jnp.sum(past * lengths[None, :], axis=1)
    return (segment, positions - start)


def rotate(values, offsets):
    half = HEAD // 2
    freq = rope_base ** (-2.0 * jnp.arange(half, dtype=jnp.float32) / HEAD)
    angle = offsets.astype(jnp.float32)[:, None] * freq[None, :]
    cosine = jnp.cos(angle)[:, None, :]
    sine = jnp.sin(angle)[:, None, :]
    first = values[..., :half]
    second = values[..., half:]
    return jnp.concatenate(
        [first * cosine - second * sine, second * cosine + first * sine], axis=-1
    )


def partners(size):
    if size & (size - 1) == 0:
        return [
            ((lambda i, s=s: jnp.bitwise_xor(i, s)), [(j, j ^ s) for j in range(size)])
            for s in range(1, size)
        ]
    return [
        ((lambda i, s=s: (i + size - s) % size), [(j, (j + s) % size) for j in range(size)])
        for s in range(1, size)
    ]

def window_attention(first, query, both, q_seg, q_pos, k_seg, k_pos, docs, interpret=False):
    rows, q_width = query.shape
    count, both_width = both.shape
    span = k_seg.shape[0]
    kv_dev = both_width // (2 * HEAD)
    group = q_width // (kv_dev * HEAD)
    scale = 1.0 / float(HEAD) ** 0.5

    def kernel(first_ref, q_ref, k_ref, v_ref, qs_ref, qp_ref, ks_ref, kp_ref, o_ref):
        start = pl.multiple_of(first_ref[0], PAGE)
        keys = k_ref[pl.ds(start, span), :]
        values = v_ref[pl.ds(start, span), :]
        qs = qs_ref[...]
        live = qs < docs - 1
        allowed = (ks_ref[...] == qs) & (kp_ref[...] <= qp_ref[...]) & live
        for g in range(group):
            q = q_ref[:, g * HEAD:(g + 1) * HEAD]
            scores = lax.dot_general(
                q, keys, (((1,), (1,)), ((), ())), preferred_element_type=jnp.float32
            ) * scale
            scores = jnp.where(allowed, scores, neg_large)
            top = jnp.max(scores, axis=1, keepdims=True)
            expo = jnp.exp(scores - top)
            denom = jnp.sum(expo, axis=1, keepdims=True)
            acc = jnp.dot(expo.astype(jnp.bfloat16), values, preferred_element_type=jnp.float32)
            out = jnp.where(live, acc / jnp.where(live, denom, 1.0), 0.0)
            o_ref[:, g * HEAD:(g + 1) * HEAD] = out.astype(o_ref.dtype)

    spec = pltpu.PrefetchScalarGridSpec(
        num_scalar_prefetch=1,
        grid=(kv_dev,),
        in_specs=[
            pl.BlockSpec((rows, group * HEAD), lambda c, f: (0, c)),
            pl.BlockSpec((count, HEAD), lambda c, f: (0, c)),
            pl.BlockSpec((count, HEAD), lambda c, f: (0, kv_dev + c)),
            pl.BlockSpec((rows, 1), lambda c, f: (0, 0)),
            pl.BlockSpec((rows, 1), lambda c, f: (0, 0)),
            pl.BlockSpec((1, span), lambda c, f: (0, 0)),
            pl.BlockSpec((1, span), lambda c, f: (0, 0)),
        ],
        out_specs=pl.BlockSpec((rows, group * HEAD), lambda c, f: (0, c)),
    )
    return pl.pallas_call(
        kernel,
        grid_spec=spec,
        out_shape=jax.ShapeDtypeStruct((rows, q_width), jnp.bfloat16),
        interpret=interpret,
    )(
        first.reshape(1).astype(jnp.int32),
        query,
        both,
        both,
        q_seg.reshape(rows, 1),
        q_pos.reshape(rows, 1),
        k_seg.reshape(1, span),
        k_pos.reshape(1, span),
    )


def local_attention(query, own_kv, q_seg, q_pos, docs, interpret=False):
    rows, q_width = query.shape
    kv_dev = own_kv.shape[1] // (2 * HEAD)
    group = q_width // (kv_dev * HEAD)
    scale = 1.0 / float(HEAD) ** 0.5

    def kernel(q_ref, k_ref, v_ref, qs_ref, qp_ref, ks_ref, kp_ref, acc_ref, top_ref, sum_ref):
        keys = k_ref[...]
        values = v_ref[...]
        qs = qs_ref[...]
        allowed = (ks_ref[...] == qs) & (kp_ref[...] <= qp_ref[...]) & (qs < docs - 1)
        for g in range(group):
            cols = slice(g * HEAD, (g + 1) * HEAD)
            scores = lax.dot_general(
                q_ref[:, cols], keys, (((1,), (1,)), ((), ())), preferred_element_type=jnp.float32
            ) * scale
            scores = jnp.where(allowed, scores, neg_large)
            top = jnp.max(scores, axis=1, keepdims=True)
            expo = jnp.exp(scores - top)
            acc_ref[:, cols] = jnp.dot(
                expo.astype(jnp.bfloat16), values, preferred_element_type=jnp.float32
            )
            top_ref[:, cols] = jnp.broadcast_to(top, (rows, HEAD))
            sum_ref[:, cols] = jnp.broadcast_to(jnp.sum(expo, axis=1, keepdims=True), (rows, HEAD))

    block = pl.BlockSpec((rows, group * HEAD), lambda c: (0, c))
    return pl.pallas_call(
        kernel,
        grid=(kv_dev,),
        in_specs=[
            block,
            pl.BlockSpec((rows, HEAD), lambda c: (0, c)),
            pl.BlockSpec((rows, HEAD), lambda c: (0, kv_dev + c)),
            pl.BlockSpec((rows, 1), lambda c: (0, 0)),
            pl.BlockSpec((rows, 1), lambda c: (0, 0)),
            pl.BlockSpec((1, rows), lambda c: (0, 0)),
            pl.BlockSpec((1, rows), lambda c: (0, 0)),
        ],
        out_specs=[block, block, block],
        out_shape=[jax.ShapeDtypeStruct((rows, q_width), jnp.float32)] * 3,
        interpret=interpret,
    )(
        query,
        own_kv,
        own_kv,
        q_seg.reshape(rows, 1),
        q_pos.reshape(rows, 1),
        q_seg.reshape(1, rows),
        q_pos.reshape(1, rows),
    )


def remote_attention(first, query, both, q_seg, k_seg, partial, docs, interpret=False):
    rows, q_width = query.shape
    count, both_width = both.shape
    span = k_seg.shape[0]
    kv_dev = both_width // (2 * HEAD)
    group = q_width // (kv_dev * HEAD)
    scale = 1.0 / float(HEAD) ** 0.5

    def kernel(first_ref, q_ref, k_ref, v_ref, qs_ref, ks_ref, acc_ref, top_ref, sum_ref, o_ref):
        start = pl.multiple_of(first_ref[0], PAGE)
        keys = k_ref[pl.ds(start, span), :]
        values = v_ref[pl.ds(start, span), :]
        qs = qs_ref[...]
        live = qs < docs - 1
        allowed = (ks_ref[...] == qs) & live
        for g in range(group):
            cols = slice(g * HEAD, (g + 1) * HEAD)
            scores = lax.dot_general(
                q_ref[:, cols], keys, (((1,), (1,)), ((), ())), preferred_element_type=jnp.float32
            ) * scale
            scores = jnp.where(allowed, scores, neg_large)
            old = top_ref[:, g * HEAD:g * HEAD + 1]
            top = jnp.maximum(old, jnp.max(scores, axis=1, keepdims=True))
            expo = jnp.where(allowed, jnp.exp(scores - top), 0.0)
            shrink = jnp.exp(old - top)
            denom = sum_ref[:, g * HEAD:g * HEAD + 1] * shrink + jnp.sum(expo, axis=1, keepdims=True)
            acc = acc_ref[:, cols] * shrink + jnp.dot(
                expo.astype(jnp.bfloat16), values, preferred_element_type=jnp.float32
            )
            out = jnp.where(live, acc / jnp.where(live, denom, 1.0), 0.0)
            o_ref[:, cols] = out.astype(o_ref.dtype)

    block = pl.BlockSpec((rows, group * HEAD), lambda c, f: (0, c))
    spec = pltpu.PrefetchScalarGridSpec(
        num_scalar_prefetch=1,
        grid=(kv_dev,),
        in_specs=[
            block,
            pl.BlockSpec((count, HEAD), lambda c, f: (0, c)),
            pl.BlockSpec((count, HEAD), lambda c, f: (0, kv_dev + c)),
            pl.BlockSpec((rows, 1), lambda c, f: (0, 0)),
            pl.BlockSpec((1, span), lambda c, f: (0, 0)),
            block,
            block,
            block,
        ],
        out_specs=block,
    )
    return pl.pallas_call(
        kernel,
        grid_spec=spec,
        out_shape=jax.ShapeDtypeStruct((rows, q_width), jnp.bfloat16),
        interpret=interpret,
    )(
        first.reshape(1).astype(jnp.int32),
        query,
        both,
        both,
        q_seg.reshape(rows, 1),
        k_seg.reshape(1, span),
        *partial,
    )

def on_device(
    tokens,
    norm_gain,
    w_query,
    w_key,
    w_value,
    query_bias,
    key_bias,
    value_bias,
    lengths,
    page_table,
):
    rows = tokens.shape[0]
    blocks = lax.axis_size("blk")
    me = lax.axis_index("blk")
    q_width = w_query.shape[1]
    kv_width = w_key.shape[1]
    kv_dev = kv_width // HEAD
    group = HEADS // KV_HEADS
    slots = rows // PAGE
    docs = lengths.shape[0]
    scale = 1.0 / float(HEAD) ** 0.5
    wide = tokens.astype(jnp.float32)
    scaled = (wide * norm_gain.astype(jnp.float32)).astype(jnp.bfloat16)
    part_sq = jnp.sum(wide * wide, axis=1)
    parts = lax.axis_size("tp")
    squares = part_sq
    for flip, perm in partners(parts):
        squares = squares + lax.ppermute(part_sq, "tp", perm)
    w_kv = jnp.concatenate([w_key, w_value], axis=1)
    width = tokens.shape[1]
    mine = lax.axis_index("tp")

    def project(chunk, source):
        return [
            jnp.dot(
                chunk,
                lax.dynamic_slice_in_dim(weight, source * width, width, 0),
                preferred_element_type=jnp.float32,
            )
            for weight in (w_kv, w_query)
        ]

    proj_kv, proj_query = project(scaled, mine)
    for flip, perm in partners(parts):
        got = lax.ppermute(scaled, "tp", perm)
        more = project(got, flip(mine))
        proj_kv = proj_kv + more[0]
        proj_query = proj_query + more[1]
    proj_key = proj_kv[:, :kv_width]
    proj_value = proj_kv[:, kv_width:]
    rstd = lax.rsqrt(squares / D + norm_eps)
    own_pos = me * rows + jnp.arange(rows, dtype=jnp.int32)
    own_seg, own_off = token_meta(own_pos, lengths)
    own_live = own_seg < docs - 1
    query = rstd[:, None] * proj_query + query_bias.astype(jnp.float32)
    key = rstd[:, None] * proj_key + key_bias.astype(jnp.float32)
    value = rstd[:, None] * proj_value + value_bias.astype(jnp.float32)
    query = (
        rotate(query.reshape(rows, q_width // HEAD, HEAD), own_off)
        .reshape(rows, q_width)
        .astype(jnp.bfloat16)
    )
    key = (
        jnp.where(own_live[:, None, None], rotate(key.reshape(rows, kv_dev, HEAD), own_off), 0.0)
        .reshape(rows, kv_width)
        .astype(jnp.bfloat16)
    )
    value = jnp.where(own_live[:, None], value, 0.0).astype(jnp.bfloat16)
    q_seg, q_off = token_meta(own_pos, lengths)
    q_live = q_seg < docs - 1
    q_grouped = query.reshape(rows, kv_dev, group, HEAD)

    own_kv = jnp.concatenate([key, value], axis=1)
    partial = local_attention(query, own_kv, q_seg, own_pos, docs)
    both = lax.all_gather(own_kv, "blk", axis=0, tiled=True)
    count = both.shape[0]
    longest = count // 2
    span = longest
    first = jnp.clip(me * rows - longest, 0, count - span)
    k_pos = first + jnp.arange(span, dtype=jnp.int32)
    k_seg, k_off = token_meta(k_pos, lengths)
    k_seg = jnp.where(k_pos < me * rows, k_seg, -1)
    mixed = remote_attention(first, query, both, q_seg, k_seg, partial, docs)
    numbers = jnp.arange(page_table.shape[0], dtype=jnp.int32)
    cache = []
    for j in range(slots):
        page = jnp.sum(jnp.where(page_table == me * slots + j, numbers, 0))
        held = lax.dynamic_slice_in_dim(both, page * PAGE, PAGE, 0)
        cache.append(jnp.stack([held[:, :kv_width], held[:, kv_width:]], axis=0))
    kv_cache = jnp.stack(cache, axis=0)
    return (mixed, kv_cache)


def solution(mesh):
    in_specs = (
        P("blk", "tp"),
        P("tp"),
        P(None, "tp"),
        P(None, "tp"),
        P(None, "tp"),
        P("tp"),
        P("tp"),
        P("tp"),
        P(),
        P(),
    )
    out_specs = (P("blk", "tp"), P("blk", None, None, "tp"))
    return jax.shard_map(
        on_device, mesh=mesh, in_specs=in_specs, out_specs=out_specs, check_vma=False
    )
```

```python
import jax
import jax.numpy as jnp
from jax import lax
from jax.experimental import pallas as pl
from jax.experimental.pallas import tpu as pltpu
from jax.sharding import PartitionSpec as P

D = 5120
HEADS = 40
KV_HEADS = 8
HEAD = 128
PAGE = 128


rope_base = 1000000.0
norm_eps = 1e-06
neg_large = -1e30


def token_meta(positions, lengths):
    ends = jnp.cumsum(lengths)
    past = (positions[:, None] >= ends[None, :]).astype(jnp.int32)
    segment = jnp.sum(past, axis=1)
    start = jnp.sum(past * lengths[None, :], axis=1)
    return (segment, positions - start)


def rotate(values, offsets):
    half = HEAD // 2
    freq = rope_base ** (-2.0 * jnp.arange(half, dtype=jnp.float32) / HEAD)
    angle = offsets.astype(jnp.float32)[:, None] * freq[None, :]
    cosine = jnp.cos(angle)[:, None, :]
    sine = jnp.sin(angle)[:, None, :]
    first = values[..., :half]
    second = values[..., half:]
    return jnp.concatenate(
        [first * cosine - second * sine, second * cosine + first * sine], axis=-1
    )


def partners(size):
    if size & (size - 1) == 0:
        return [
            ((lambda i, s=s: jnp.bitwise_xor(i, s)), [(j, j ^ s) for j in range(size)])
            for s in range(1, size)
        ]
    return [
        ((lambda i, s=s: (i + size - s) % size), [(j, (j + s) % size) for j in range(size)])
        for s in range(1, size)
    ]

def window_attention(first, query, both, q_seg, q_pos, k_seg, k_pos, docs, interpret=False):
    rows, q_width = query.shape
    count, both_width = both.shape
    span = k_seg.shape[0]
    kv_dev = both_width // (2 * HEAD)
    group = q_width // (kv_dev * HEAD)
    scale = 1.0 / float(HEAD) ** 0.5

    def kernel(first_ref, q_ref, k_ref, v_ref, qs_ref, qp_ref, ks_ref, kp_ref, o_ref):
        start = pl.multiple_of(first_ref[0], PAGE)
        keys = k_ref[pl.ds(start, span), :]
        values = v_ref[pl.ds(start, span), :]
        qs = qs_ref[...]
        live = qs < docs - 1
        allowed = (ks_ref[...] == qs) & (kp_ref[...] <= qp_ref[...]) & live
        for g in range(group):
            q = q_ref[:, g * HEAD:(g + 1) * HEAD]
            scores = lax.dot_general(
                q, keys, (((1,), (1,)), ((), ())), preferred_element_type=jnp.float32
            )
            scores = jnp.where(allowed, scores, neg_large)
            top = jnp.max(scores, axis=1, keepdims=True)
            expo = jnp.exp((scores - top) * scale)
            denom = jnp.sum(expo, axis=1, keepdims=True)
            acc = jnp.dot(expo.astype(jnp.bfloat16), values, preferred_element_type=jnp.float32)
            out = jnp.where(live, acc / jnp.where(live, denom, 1.0), 0.0)
            o_ref[:, g * HEAD:(g + 1) * HEAD] = out.astype(o_ref.dtype)

    spec = pltpu.PrefetchScalarGridSpec(
        num_scalar_prefetch=1,
        grid=(kv_dev,),
        in_specs=[
            pl.BlockSpec((rows, group * HEAD), lambda c, f: (0, c)),
            pl.BlockSpec((count, HEAD), lambda c, f: (0, c)),
            pl.BlockSpec((count, HEAD), lambda c, f: (0, kv_dev + c)),
            pl.BlockSpec((rows, 1), lambda c, f: (0, 0)),
            pl.BlockSpec((rows, 1), lambda c, f: (0, 0)),
            pl.BlockSpec((1, span), lambda c, f: (0, 0)),
            pl.BlockSpec((1, span), lambda c, f: (0, 0)),
        ],
        out_specs=pl.BlockSpec((rows, group * HEAD), lambda c, f: (0, c)),
    )
    return pl.pallas_call(
        kernel,
        grid_spec=spec,
        out_shape=jax.ShapeDtypeStruct((rows, q_width), jnp.bfloat16),
        interpret=interpret,
    )(
        first.reshape(1).astype(jnp.int32),
        query,
        both,
        both,
        q_seg.reshape(rows, 1),
        q_pos.reshape(rows, 1),
        k_seg.reshape(1, span),
        k_pos.reshape(1, span),
    )

def on_device(
    tokens,
    norm_gain,
    w_query,
    w_key,
    w_value,
    query_bias,
    key_bias,
    value_bias,
    lengths,
    page_table,
):
    rows = tokens.shape[0]
    blocks = lax.axis_size("blk")
    me = lax.axis_index("blk")
    q_width = w_query.shape[1]
    kv_width = w_key.shape[1]
    kv_dev = kv_width // HEAD
    group = HEADS // KV_HEADS
    slots = rows // PAGE
    docs = lengths.shape[0]
    scale = 1.0 / float(HEAD) ** 0.5
    wide = tokens.astype(jnp.float32)
    scaled = (wide * norm_gain.astype(jnp.float32)).astype(jnp.bfloat16)
    part_sq = jnp.sum(wide * wide, axis=1)
    parts = lax.axis_size("tp")
    squares = part_sq
    for flip, perm in partners(parts):
        squares = squares + lax.ppermute(part_sq, "tp", perm)
    w_kv = jnp.concatenate([w_key, w_value], axis=1)
    width = tokens.shape[1]
    mine = lax.axis_index("tp")

    def project(chunk, source):
        return [
            jnp.dot(
                chunk,
                lax.dynamic_slice_in_dim(weight, source * width, width, 0),
                preferred_element_type=jnp.float32,
            )
            for weight in (w_kv, w_query)
        ]

    proj_kv, proj_query = project(scaled, mine)
    for flip, perm in partners(parts):
        got = lax.ppermute(scaled, "tp", perm)
        more = project(got, flip(mine))
        proj_kv = proj_kv + more[0]
        proj_query = proj_query + more[1]
    proj_key = proj_kv[:, :kv_width]
    proj_value = proj_kv[:, kv_width:]
    rstd = lax.rsqrt(squares / D + norm_eps)
    own_pos = me * rows + jnp.arange(rows, dtype=jnp.int32)
    own_seg, own_off = token_meta(own_pos, lengths)
    own_live = own_seg < docs - 1
    query = rstd[:, None] * proj_query + query_bias.astype(jnp.float32)
    key = rstd[:, None] * proj_key + key_bias.astype(jnp.float32)
    value = rstd[:, None] * proj_value + value_bias.astype(jnp.float32)
    query = (
        rotate(query.reshape(rows, q_width // HEAD, HEAD), own_off)
        .reshape(rows, q_width)
        .astype(jnp.bfloat16)
    )
    key = (
        jnp.where(own_live[:, None, None], rotate(key.reshape(rows, kv_dev, HEAD), own_off), 0.0)
        .reshape(rows, kv_width)
        .astype(jnp.bfloat16)
    )
    value = jnp.where(own_live[:, None], value, 0.0).astype(jnp.bfloat16)
    q_seg, q_off = token_meta(own_pos, lengths)
    q_live = q_seg < docs - 1
    q_grouped = query.reshape(rows, kv_dev, group, HEAD)

    both = lax.all_gather(jnp.concatenate([key, value], axis=1), "blk", axis=0, tiled=True)
    count = both.shape[0]
    longest = count // 2
    span = min(count, longest + rows)
    first = jnp.clip(me * rows - longest, 0, count - span)
    k_pos = first + jnp.arange(span, dtype=jnp.int32)
    k_seg, k_off = token_meta(k_pos, lengths)
    mixed = window_attention(first, query, both, q_seg, own_pos, k_seg, k_pos, docs)
    numbers = jnp.arange(page_table.shape[0], dtype=jnp.int32)
    cache = []
    for j in range(slots):
        page = jnp.sum(jnp.where(page_table == me * slots + j, numbers, 0))
        held = lax.dynamic_slice_in_dim(both, page * PAGE, PAGE, 0)
        cache.append(jnp.stack([held[:, :kv_width], held[:, kv_width:]], axis=0))
    kv_cache = jnp.stack(cache, axis=0)
    return (mixed, kv_cache)


def solution(mesh):
    in_specs = (
        P("blk", "tp"),
        P("tp"),
        P(None, "tp"),
        P(None, "tp"),
        P(None, "tp"),
        P("tp"),
        P("tp"),
        P("tp"),
        P(),
        P(),
    )
    out_specs = (P("blk", "tp"), P("blk", None, None, "tp"))
    return jax.shard_map(
        on_device, mesh=mesh, in_specs=in_specs, out_specs=out_specs, check_vma=False
    )
```

```python
import jax
import jax.numpy as jnp
from jax import lax
from jax.experimental import pallas as pl
from jax.experimental.pallas import tpu as pltpu
from jax.sharding import PartitionSpec as P

D = 5120
HEADS = 40
KV_HEADS = 8
HEAD = 128
PAGE = 128


rope_base = 1000000.0
norm_eps = 1e-06
neg_large = -1e30


def token_meta(positions, lengths):
    ends = jnp.cumsum(lengths)
    past = (positions[:, None] >= ends[None, :]).astype(jnp.int32)
    segment = jnp.sum(past, axis=1)
    start = jnp.sum(past * lengths[None, :], axis=1)
    return (segment, positions - start)


def rotate(values, offsets):
    half = HEAD // 2
    freq = rope_base ** (-2.0 * jnp.arange(half, dtype=jnp.float32) / HEAD)
    angle = offsets.astype(jnp.float32)[:, None] * freq[None, :]
    cosine = jnp.cos(angle)[:, None, :]
    sine = jnp.sin(angle)[:, None, :]
    first = values[..., :half]
    second = values[..., half:]
    return jnp.concatenate(
        [first * cosine - second * sine, second * cosine + first * sine], axis=-1
    )


def partners(size):
    if size & (size - 1) == 0:
        return [
            ((lambda i, s=s: jnp.bitwise_xor(i, s)), [(j, j ^ s) for j in range(size)])
            for s in range(1, size)
        ]
    return [
        ((lambda i, s=s: (i + size - s) % size), [(j, (j + s) % size) for j in range(size)])
        for s in range(1, size)
    ]

def window_attention(first, query, both, q_seg, q_pos, k_seg, k_pos, docs, pages, interpret=False):
    rows, q_width = query.shape
    count, both_width = both.shape
    span = k_seg.shape[0]
    kv_dev = both_width // (2 * HEAD)
    group = q_width // (kv_dev * HEAD)
    scale = 1.0 / float(HEAD) ** 0.5

    slots = pages.shape[0]

    def kernel(first_ref, page_ref, q_ref, k_ref, v_ref, qs_ref, qp_ref, ks_ref, kp_ref, o_ref, c_ref):
        for j in range(slots):
            row = pl.multiple_of(page_ref[j] * PAGE, PAGE)
            c_ref[j, 0] = k_ref[pl.ds(row, PAGE), :]
            c_ref[j, 1] = v_ref[pl.ds(row, PAGE), :]
        start = pl.multiple_of(first_ref[0], PAGE)
        keys = k_ref[pl.ds(start, span), :]
        values = v_ref[pl.ds(start, span), :]
        qs = qs_ref[...]
        live = qs < docs - 1
        allowed = (ks_ref[...] == qs) & (kp_ref[...] <= qp_ref[...]) & live
        for g in range(group):
            q = q_ref[:, g * HEAD:(g + 1) * HEAD]
            scores = lax.dot_general(
                q, keys, (((1,), (1,)), ((), ())), preferred_element_type=jnp.float32
            ) * scale
            scores = jnp.where(allowed, scores, neg_large)
            top = jnp.max(scores, axis=1, keepdims=True)
            expo = jnp.exp(scores - top)
            denom = jnp.sum(expo, axis=1, keepdims=True)
            acc = jnp.dot(expo.astype(jnp.bfloat16), values, preferred_element_type=jnp.float32)
            out = jnp.where(live, acc / jnp.where(live, denom, 1.0), 0.0)
            o_ref[:, g * HEAD:(g + 1) * HEAD] = out.astype(o_ref.dtype)

    spec = pltpu.PrefetchScalarGridSpec(
        num_scalar_prefetch=2,
        grid=(kv_dev,),
        in_specs=[
            pl.BlockSpec((rows, group * HEAD), lambda c, f, p: (0, c)),
            pl.BlockSpec((count, HEAD), lambda c, f, p: (0, c)),
            pl.BlockSpec((count, HEAD), lambda c, f, p: (0, kv_dev + c)),
            pl.BlockSpec((rows, 1), lambda c, f, p: (0, 0)),
            pl.BlockSpec((rows, 1), lambda c, f, p: (0, 0)),
            pl.BlockSpec((1, span), lambda c, f, p: (0, 0)),
            pl.BlockSpec((1, span), lambda c, f, p: (0, 0)),
        ],
        out_specs=[
            pl.BlockSpec((rows, group * HEAD), lambda c, f, p: (0, c)),
            pl.BlockSpec((slots, 2, PAGE, HEAD), lambda c, f, p: (0, 0, 0, c)),
        ],
    )
    return pl.pallas_call(
        kernel,
        grid_spec=spec,
        out_shape=[
            jax.ShapeDtypeStruct((rows, q_width), jnp.bfloat16),
            jax.ShapeDtypeStruct((slots, 2, PAGE, kv_dev * HEAD), both.dtype),
        ],
        interpret=interpret,
    )(
        first.reshape(1).astype(jnp.int32),
        pages.astype(jnp.int32),
        query,
        both,
        both,
        q_seg.reshape(rows, 1),
        q_pos.reshape(rows, 1),
        k_seg.reshape(1, span),
        k_pos.reshape(1, span),
    )

def on_device(
    tokens,
    norm_gain,
    w_query,
    w_key,
    w_value,
    query_bias,
    key_bias,
    value_bias,
    lengths,
    page_table,
):
    rows = tokens.shape[0]
    blocks = lax.axis_size("blk")
    me = lax.axis_index("blk")
    q_width = w_query.shape[1]
    kv_width = w_key.shape[1]
    kv_dev = kv_width // HEAD
    group = HEADS // KV_HEADS
    slots = rows // PAGE
    docs = lengths.shape[0]
    scale = 1.0 / float(HEAD) ** 0.5
    wide = tokens.astype(jnp.float32)
    scaled = (wide * norm_gain.astype(jnp.float32)).astype(jnp.bfloat16)
    part_sq = jnp.sum(wide * wide, axis=1)
    parts = lax.axis_size("tp")
    squares = part_sq
    for flip, perm in partners(parts):
        squares = squares + lax.ppermute(part_sq, "tp", perm)
    w_kv = jnp.concatenate([w_key, w_value], axis=1)
    width = tokens.shape[1]
    mine = lax.axis_index("tp")

    def project(chunk, source):
        return [
            jnp.dot(
                chunk,
                lax.dynamic_slice_in_dim(weight, source * width, width, 0),
                preferred_element_type=jnp.float32,
            )
            for weight in (w_kv, w_query)
        ]

    proj_kv, proj_query = project(scaled, mine)
    for flip, perm in partners(parts):
        got = lax.ppermute(scaled, "tp", perm)
        more = project(got, flip(mine))
        proj_kv = proj_kv + more[0]
        proj_query = proj_query + more[1]
    proj_key = proj_kv[:, :kv_width]
    proj_value = proj_kv[:, kv_width:]
    rstd = lax.rsqrt(squares / D + norm_eps)
    own_pos = me * rows + jnp.arange(rows, dtype=jnp.int32)
    own_seg, own_off = token_meta(own_pos, lengths)
    own_live = own_seg < docs - 1
    query = rstd[:, None] * proj_query + query_bias.astype(jnp.float32)
    key = rstd[:, None] * proj_key + key_bias.astype(jnp.float32)
    value = rstd[:, None] * proj_value + value_bias.astype(jnp.float32)
    query = (
        rotate(query.reshape(rows, q_width // HEAD, HEAD), own_off)
        .reshape(rows, q_width)
        .astype(jnp.bfloat16)
    )
    key = (
        jnp.where(own_live[:, None, None], rotate(key.reshape(rows, kv_dev, HEAD), own_off), 0.0)
        .reshape(rows, kv_width)
        .astype(jnp.bfloat16)
    )
    value = jnp.where(own_live[:, None], value, 0.0).astype(jnp.bfloat16)
    q_seg, q_off = token_meta(own_pos, lengths)
    q_live = q_seg < docs - 1
    q_grouped = query.reshape(rows, kv_dev, group, HEAD)

    both = lax.all_gather(jnp.concatenate([key, value], axis=1), "blk", axis=0, tiled=True)
    count = both.shape[0]
    longest = count // 2
    span = min(count, longest + rows)
    first = jnp.clip(me * rows - longest, 0, count - span)
    k_pos = first + jnp.arange(span, dtype=jnp.int32)
    k_seg, k_off = token_meta(k_pos, lengths)
    numbers = jnp.arange(page_table.shape[0], dtype=jnp.int32)
    pages = jnp.stack(
        [jnp.sum(jnp.where(page_table == me * slots + j, numbers, 0)) for j in range(slots)]
    )
    pages = jnp.clip(pages, 0, count // PAGE - 1)
    mixed, kv_cache = window_attention(
        first, query, both, q_seg, own_pos, k_seg, k_pos, docs, pages
    )
    return (mixed, kv_cache)


def solution(mesh):
    in_specs = (
        P("blk", "tp"),
        P("tp"),
        P(None, "tp"),
        P(None, "tp"),
        P(None, "tp"),
        P("tp"),
        P("tp"),
        P("tp"),
        P(),
        P(),
    )
    out_specs = (P("blk", "tp"), P("blk", None, None, "tp"))
    return jax.shard_map(
        on_device, mesh=mesh, in_specs=in_specs, out_specs=out_specs, check_vma=False
    )
```

```python
import jax
import jax.numpy as jnp
from jax import lax
from jax.experimental import pallas as pl
from jax.experimental.pallas import tpu as pltpu
from jax.sharding import PartitionSpec as P

D = 5120
HEADS = 40
KV_HEADS = 8
HEAD = 128
PAGE = 128


rope_base = 1000000.0
norm_eps = 1e-06
neg_large = -1e30


def token_meta(positions, lengths):
    ends = jnp.cumsum(lengths)
    past = (positions[:, None] >= ends[None, :]).astype(jnp.int32)
    segment = jnp.sum(past, axis=1)
    start = jnp.sum(past * lengths[None, :], axis=1)
    return (segment, positions - start)


def rotate(values, offsets):
    half = HEAD // 2
    freq = rope_base ** (-2.0 * jnp.arange(half, dtype=jnp.float32) / HEAD)
    angle = offsets.astype(jnp.float32)[:, None] * freq[None, :]
    cosine = jnp.cos(angle)[:, None, :]
    sine = jnp.sin(angle)[:, None, :]
    first = values[..., :half]
    second = values[..., half:]
    return jnp.concatenate(
        [first * cosine - second * sine, second * cosine + first * sine], axis=-1
    )


def partners(size):
    if size & (size - 1) == 0:
        return [
            ((lambda i, s=s: jnp.bitwise_xor(i, s)), [(j, j ^ s) for j in range(size)])
            for s in range(1, size)
        ]
    return [
        ((lambda i, s=s: (i + size - s) % size), [(j, (j + s) % size) for j in range(size)])
        for s in range(1, size)
    ]

def window_attention(first, query, both, q_seg, q_pos, k_seg, k_pos, docs, pages, interpret=False):
    rows, q_width = query.shape
    count, both_width = both.shape
    span = k_seg.shape[0]
    kv_dev = both_width // (2 * HEAD)
    group = q_width // (kv_dev * HEAD)
    scale = 1.0 / float(HEAD) ** 0.5

    slots = pages.shape[0]

    def kernel(first_ref, page_ref, q_ref, k_ref, v_ref, qs_ref, qp_ref, ks_ref, kp_ref, o_ref, c_ref):
        for j in range(slots):
            row = pl.multiple_of(page_ref[j] * PAGE, PAGE)
            c_ref[j, 0] = k_ref[pl.ds(row, PAGE), :]
            c_ref[j, 1] = v_ref[pl.ds(row, PAGE), :]
        start = pl.multiple_of(first_ref[0], PAGE)
        keys = k_ref[pl.ds(start, span), :]
        values = v_ref[pl.ds(start, span), :]
        qs = qs_ref[...]
        live = qs < docs - 1
        allowed = (ks_ref[...] == qs) & (kp_ref[...] <= qp_ref[...]) & live
        for g in range(group):
            q = q_ref[:, g * HEAD:(g + 1) * HEAD]
            scores = lax.dot_general(
                q, keys, (((1,), (1,)), ((), ())), preferred_element_type=jnp.float32
            ) * scale
            scores = jnp.where(allowed, scores, neg_large)
            top = jnp.max(scores, axis=1, keepdims=True)
            expo = jnp.exp(scores - top)
            denom = jnp.sum(expo, axis=1, keepdims=True)
            acc = jnp.dot(expo.astype(jnp.bfloat16), values, preferred_element_type=jnp.float32)
            out = jnp.where(live, acc / jnp.where(live, denom, 1.0), 0.0)
            o_ref[:, g * HEAD:(g + 1) * HEAD] = out.astype(o_ref.dtype)

    spec = pltpu.PrefetchScalarGridSpec(
        num_scalar_prefetch=2,
        grid=(kv_dev,),
        in_specs=[
            pl.BlockSpec((rows, group * HEAD), lambda c, f, p: (0, c)),
            pl.BlockSpec((count, HEAD), lambda c, f, p: (0, c)),
            pl.BlockSpec((count, HEAD), lambda c, f, p: (0, kv_dev + c)),
            pl.BlockSpec((rows, 1), lambda c, f, p: (0, 0)),
            pl.BlockSpec((rows, 1), lambda c, f, p: (0, 0)),
            pl.BlockSpec((1, span), lambda c, f, p: (0, 0)),
            pl.BlockSpec((1, span), lambda c, f, p: (0, 0)),
        ],
        out_specs=[
            pl.BlockSpec((rows, group * HEAD), lambda c, f, p: (0, c)),
            pl.BlockSpec((slots, 2, PAGE, HEAD), lambda c, f, p: (0, 0, 0, c)),
        ],
    )
    return pl.pallas_call(
        kernel,
        grid_spec=spec,
        out_shape=[
            jax.ShapeDtypeStruct((rows, q_width), jnp.bfloat16),
            jax.ShapeDtypeStruct((slots, 2, PAGE, kv_dev * HEAD), both.dtype),
        ],
        interpret=interpret,
    )(
        first.reshape(1).astype(jnp.int32),
        pages.astype(jnp.int32),
        query,
        both,
        both,
        q_seg.reshape(rows, 1),
        q_pos.reshape(rows, 1),
        k_seg.reshape(1, span),
        k_pos.reshape(1, span),
    )

def on_device(
    tokens,
    norm_gain,
    w_query,
    w_key,
    w_value,
    query_bias,
    key_bias,
    value_bias,
    lengths,
    page_table,
):
    rows = tokens.shape[0]
    blocks = lax.axis_size("blk")
    me = lax.axis_index("blk")
    q_width = w_query.shape[1]
    kv_width = w_key.shape[1]
    kv_dev = kv_width // HEAD
    group = HEADS // KV_HEADS
    slots = rows // PAGE
    docs = lengths.shape[0]
    scale = 1.0 / float(HEAD) ** 0.5
    wide = tokens.astype(jnp.float32)
    scaled = (wide * norm_gain.astype(jnp.float32)).astype(jnp.bfloat16)
    part_sq = jnp.sum(wide * wide, axis=1)
    parts = lax.axis_size("tp")
    squares = part_sq
    for flip, perm in partners(parts):
        squares = squares + lax.ppermute(part_sq, "tp", perm)
    w_kv = jnp.concatenate([w_key, w_value], axis=1)
    width = tokens.shape[1]
    mine = lax.axis_index("tp")

    def project(chunk, source):
        return [
            jnp.dot(
                chunk,
                lax.dynamic_slice_in_dim(weight, source * width, width, 0),
                preferred_element_type=jnp.float32,
            )
            for weight in (w_kv, w_query)
        ]

    proj_kv, proj_query = project(scaled, mine)
    received = []
    w_far = []
    for flip, perm in partners(parts):
        got = lax.ppermute(scaled, "tp", perm)
        received.append(got)
        w_far.append(lax.dynamic_slice_in_dim(w_kv, flip(mine) * width, width, 0))
        proj_query = proj_query + jnp.dot(
            got,
            lax.dynamic_slice_in_dim(w_query, flip(mine) * width, width, 0),
            preferred_element_type=jnp.float32,
        )
    proj_kv = proj_kv + jnp.dot(
        jnp.concatenate(received, axis=1),
        jnp.concatenate(w_far, axis=0),
        preferred_element_type=jnp.float32,
    )
    proj_key = proj_kv[:, :kv_width]
    proj_value = proj_kv[:, kv_width:]
    rstd = lax.rsqrt(squares / D + norm_eps)
    own_pos = me * rows + jnp.arange(rows, dtype=jnp.int32)
    own_seg, own_off = token_meta(own_pos, lengths)
    own_live = own_seg < docs - 1
    query = rstd[:, None] * proj_query + query_bias.astype(jnp.float32)
    key = rstd[:, None] * proj_key + key_bias.astype(jnp.float32)
    value = rstd[:, None] * proj_value + value_bias.astype(jnp.float32)
    query = (
        rotate(query.reshape(rows, q_width // HEAD, HEAD), own_off)
        .reshape(rows, q_width)
        .astype(jnp.bfloat16)
    )
    key = (
        jnp.where(own_live[:, None, None], rotate(key.reshape(rows, kv_dev, HEAD), own_off), 0.0)
        .reshape(rows, kv_width)
        .astype(jnp.bfloat16)
    )
    value = jnp.where(own_live[:, None], value, 0.0).astype(jnp.bfloat16)
    q_seg, q_off = token_meta(own_pos, lengths)
    q_live = q_seg < docs - 1
    q_grouped = query.reshape(rows, kv_dev, group, HEAD)

    both = lax.all_gather(jnp.concatenate([key, value], axis=1), "blk", axis=0, tiled=True)
    count = both.shape[0]
    longest = count // 2
    span = min(count, longest + rows)
    first = jnp.clip(me * rows - longest, 0, count - span)
    k_pos = first + jnp.arange(span, dtype=jnp.int32)
    k_seg, k_off = token_meta(k_pos, lengths)
    numbers = jnp.arange(page_table.shape[0], dtype=jnp.int32)
    pages = jnp.stack(
        [jnp.sum(jnp.where(page_table == me * slots + j, numbers, 0)) for j in range(slots)]
    )
    pages = jnp.clip(pages, 0, count // PAGE - 1)
    mixed, kv_cache = window_attention(
        first, query, both, q_seg, own_pos, k_seg, k_pos, docs, pages
    )
    return (mixed, kv_cache)


def solution(mesh):
    in_specs = (
        P("blk", "tp"),
        P("tp"),
        P(None, "tp"),
        P(None, "tp"),
        P(None, "tp"),
        P("tp"),
        P("tp"),
        P("tp"),
        P(),
        P(),
    )
    out_specs = (P("blk", "tp"), P("blk", None, None, "tp"))
    return jax.shard_map(
        on_device, mesh=mesh, in_specs=in_specs, out_specs=out_specs, check_vma=False
    )
```

```python
import jax
import jax.numpy as jnp
from jax import lax
from jax.experimental import pallas as pl
from jax.experimental.pallas import tpu as pltpu
from jax.sharding import PartitionSpec as P

D = 5120
HEADS = 40
KV_HEADS = 8
HEAD = 128
PAGE = 128


rope_base = 1000000.0
norm_eps = 1e-06
neg_large = -1e30


def token_meta(positions, lengths):
    ends = jnp.cumsum(lengths)
    past = (positions[:, None] >= ends[None, :]).astype(jnp.int32)
    segment = jnp.sum(past, axis=1)
    start = jnp.sum(past * lengths[None, :], axis=1)
    return (segment, positions - start)


def rotate(values, offsets):
    half = HEAD // 2
    freq = rope_base ** (-2.0 * jnp.arange(half, dtype=jnp.float32) / HEAD)
    angle = offsets.astype(jnp.float32)[:, None] * freq[None, :]
    cosine = jnp.cos(angle)[:, None, :]
    sine = jnp.sin(angle)[:, None, :]
    first = values[..., :half]
    second = values[..., half:]
    return jnp.concatenate(
        [first * cosine - second * sine, second * cosine + first * sine], axis=-1
    )


def partners(size):
    if size & (size - 1) == 0:
        return [
            ((lambda i, s=s: jnp.bitwise_xor(i, s)), [(j, j ^ s) for j in range(size)])
            for s in range(1, size)
        ]
    return [
        ((lambda i, s=s: (i + size - s) % size), [(j, (j + s) % size) for j in range(size)])
        for s in range(1, size)
    ]

def window_attention(first, query, both, q_seg, q_pos, k_seg, k_pos, docs, pages, interpret=False):
    rows, q_width = query.shape
    count, both_width = both.shape
    span = k_seg.shape[0]
    kv_dev = both_width // (2 * HEAD)
    group = q_width // (kv_dev * HEAD)
    scale = 1.0 / float(HEAD) ** 0.5

    slots = pages.shape[0]

    def kernel(first_ref, page_ref, q_ref, k_ref, v_ref, qs_ref, qp_ref, ks_ref, kp_ref, o_ref, c_ref):
        for j in range(slots):
            row = pl.multiple_of(page_ref[j] * PAGE, PAGE)
            c_ref[j, 0] = k_ref[pl.ds(row, PAGE), :]
            c_ref[j, 1] = v_ref[pl.ds(row, PAGE), :]
        start = pl.multiple_of(first_ref[0], PAGE)
        keys = k_ref[pl.ds(start, span), :]
        values = v_ref[pl.ds(start, span), :]
        qs = qs_ref[...]
        live = qs < docs - 1
        allowed = (ks_ref[...] == qs) & (kp_ref[...] <= qp_ref[...]) & live
        for g in range(group):
            q = q_ref[:, g * HEAD:(g + 1) * HEAD]
            scores = lax.dot_general(
                q, keys, (((1,), (1,)), ((), ())), preferred_element_type=jnp.float32
            ) * scale
            scores = jnp.where(allowed, scores, neg_large)
            top = jnp.max(scores, axis=1, keepdims=True)
            expo = jnp.exp(scores - top)
            denom = jnp.sum(expo, axis=1, keepdims=True)
            acc = jnp.dot(expo.astype(jnp.bfloat16), values, preferred_element_type=jnp.float32)
            out = jnp.where(live, acc / jnp.where(live, denom, 1.0), 0.0)
            o_ref[:, g * HEAD:(g + 1) * HEAD] = out.astype(o_ref.dtype)

    spec = pltpu.PrefetchScalarGridSpec(
        num_scalar_prefetch=2,
        grid=(kv_dev,),
        in_specs=[
            pl.BlockSpec((rows, group * HEAD), lambda c, f, p: (0, c)),
            pl.BlockSpec((count, HEAD), lambda c, f, p: (0, c)),
            pl.BlockSpec((count, HEAD), lambda c, f, p: (0, kv_dev + c)),
            pl.BlockSpec((rows, 1), lambda c, f, p: (0, 0)),
            pl.BlockSpec((rows, 1), lambda c, f, p: (0, 0)),
            pl.BlockSpec((1, span), lambda c, f, p: (0, 0)),
            pl.BlockSpec((1, span), lambda c, f, p: (0, 0)),
        ],
        out_specs=[
            pl.BlockSpec((rows, group * HEAD), lambda c, f, p: (0, c)),
            pl.BlockSpec((slots, 2, PAGE, HEAD), lambda c, f, p: (0, 0, 0, c)),
        ],
    )
    return pl.pallas_call(
        kernel,
        grid_spec=spec,
        out_shape=[
            jax.ShapeDtypeStruct((rows, q_width), jnp.bfloat16),
            jax.ShapeDtypeStruct((slots, 2, PAGE, kv_dev * HEAD), both.dtype),
        ],
        interpret=interpret,
    )(
        first.reshape(1).astype(jnp.int32),
        pages.astype(jnp.int32),
        query,
        both,
        both,
        q_seg.reshape(rows, 1),
        q_pos.reshape(rows, 1),
        k_seg.reshape(1, span),
        k_pos.reshape(1, span),
    )

def on_device(
    tokens,
    norm_gain,
    w_query,
    w_key,
    w_value,
    query_bias,
    key_bias,
    value_bias,
    lengths,
    page_table,
):
    rows = tokens.shape[0]
    blocks = lax.axis_size("blk")
    me = lax.axis_index("blk")
    q_width = w_query.shape[1]
    kv_width = w_key.shape[1]
    kv_dev = kv_width // HEAD
    group = HEADS // KV_HEADS
    slots = rows // PAGE
    docs = lengths.shape[0]
    scale = 1.0 / float(HEAD) ** 0.5
    wide = tokens.astype(jnp.float32)
    scaled = (wide * norm_gain.astype(jnp.float32)).astype(jnp.bfloat16)
    part_sq = jnp.sum(wide * wide, axis=1)
    parts = lax.axis_size("tp")
    squares = part_sq
    for flip, perm in partners(parts):
        squares = squares + lax.ppermute(part_sq, "tp", perm)
    w_kv = jnp.concatenate([w_key, w_value], axis=1)
    width = tokens.shape[1]
    mine = lax.axis_index("tp")

    def project(chunk, source):
        return [
            jnp.dot(
                chunk,
                lax.dynamic_slice_in_dim(weight, source * width, width, 0),
                preferred_element_type=jnp.float32,
            )
            for weight in (w_kv, w_query)
        ]

    proj_kv, proj_query = project(scaled, mine)
    for flip, perm in partners(parts):
        got = lax.ppermute(scaled, "tp", perm)
        w_far = lax.optimization_barrier(
            lax.dynamic_slice_in_dim(w_kv, flip(mine) * width, width, 0)
        )
        proj_kv = proj_kv + jnp.dot(got, w_far, preferred_element_type=jnp.float32)
        proj_query = proj_query + jnp.dot(
            got,
            lax.dynamic_slice_in_dim(w_query, flip(mine) * width, width, 0),
            preferred_element_type=jnp.float32,
        )
    proj_key = proj_kv[:, :kv_width]
    proj_value = proj_kv[:, kv_width:]
    rstd = lax.rsqrt(squares / D + norm_eps)
    own_pos = me * rows + jnp.arange(rows, dtype=jnp.int32)
    own_seg, own_off = token_meta(own_pos, lengths)
    own_live = own_seg < docs - 1
    query = rstd[:, None] * proj_query + query_bias.astype(jnp.float32)
    key = rstd[:, None] * proj_key + key_bias.astype(jnp.float32)
    value = rstd[:, None] * proj_value + value_bias.astype(jnp.float32)
    query = (
        rotate(query.reshape(rows, q_width // HEAD, HEAD), own_off)
        .reshape(rows, q_width)
        .astype(jnp.bfloat16)
    )
    key = (
        jnp.where(own_live[:, None, None], rotate(key.reshape(rows, kv_dev, HEAD), own_off), 0.0)
        .reshape(rows, kv_width)
        .astype(jnp.bfloat16)
    )
    value = jnp.where(own_live[:, None], value, 0.0).astype(jnp.bfloat16)
    q_seg, q_off = token_meta(own_pos, lengths)
    q_live = q_seg < docs - 1
    q_grouped = query.reshape(rows, kv_dev, group, HEAD)

    both = lax.all_gather(jnp.concatenate([key, value], axis=1), "blk", axis=0, tiled=True)
    count = both.shape[0]
    longest = count // 2
    span = min(count, longest + rows)
    first = jnp.clip(me * rows - longest, 0, count - span)
    k_pos = first + jnp.arange(span, dtype=jnp.int32)
    k_seg, k_off = token_meta(k_pos, lengths)
    numbers = jnp.arange(page_table.shape[0], dtype=jnp.int32)
    pages = jnp.stack(
        [jnp.sum(jnp.where(page_table == me * slots + j, numbers, 0)) for j in range(slots)]
    )
    pages = jnp.clip(pages, 0, count // PAGE - 1)
    mixed, kv_cache = window_attention(
        first, query, both, q_seg, own_pos, k_seg, k_pos, docs, pages
    )
    return (mixed, kv_cache)


def solution(mesh):
    in_specs = (
        P("blk", "tp"),
        P("tp"),
        P(None, "tp"),
        P(None, "tp"),
        P(None, "tp"),
        P("tp"),
        P("tp"),
        P("tp"),
        P(),
        P(),
    )
    out_specs = (P("blk", "tp"), P("blk", None, None, "tp"))
    return jax.shard_map(
        on_device, mesh=mesh, in_specs=in_specs, out_specs=out_specs, check_vma=False
    )
```

```python
import jax
import jax.numpy as jnp
from jax import lax
from jax.experimental import pallas as pl
from jax.experimental.pallas import tpu as pltpu
from jax.sharding import PartitionSpec as P

D = 5120
HEADS = 40
KV_HEADS = 8
HEAD = 128
PAGE = 128


rope_base = 1000000.0
norm_eps = 1e-06
neg_large = -1e30


def token_meta(positions, lengths):
    ends = jnp.cumsum(lengths)
    past = (positions[:, None] >= ends[None, :]).astype(jnp.int32)
    segment = jnp.sum(past, axis=1)
    start = jnp.sum(past * lengths[None, :], axis=1)
    return (segment, positions - start)


def rotate(values, offsets):
    half = HEAD // 2
    freq = rope_base ** (-2.0 * jnp.arange(half, dtype=jnp.float32) / HEAD)
    angle = offsets.astype(jnp.float32)[:, None] * freq[None, :]
    cosine = jnp.cos(angle)[:, None, :]
    sine = jnp.sin(angle)[:, None, :]
    first = values[..., :half]
    second = values[..., half:]
    return jnp.concatenate(
        [first * cosine - second * sine, second * cosine + first * sine], axis=-1
    )


def partners(size):
    if size & (size - 1) == 0:
        return [
            ((lambda i, s=s: jnp.bitwise_xor(i, s)), [(j, j ^ s) for j in range(size)])
            for s in range(1, size)
        ]
    return [
        ((lambda i, s=s: (i + size - s) % size), [(j, (j + s) % size) for j in range(size)])
        for s in range(1, size)
    ]

def window_attention(first, query, both, q_seg, q_pos, k_seg, k_pos, docs, pages, interpret=False):
    rows, q_width = query.shape
    count, both_width = both.shape
    span = k_seg.shape[0]
    kv_dev = both_width // (2 * HEAD)
    group = q_width // (kv_dev * HEAD)
    scale = 1.0 / float(HEAD) ** 0.5

    slots = pages.shape[0]

    def kernel(first_ref, page_ref, q_ref, k_ref, v_ref, qs_ref, qp_ref, ks_ref, kp_ref, o_ref, c_ref):
        for j in range(slots):
            row = pl.multiple_of(page_ref[j] * PAGE, PAGE)
            c_ref[j, 0] = k_ref[pl.ds(row, PAGE), :]
            c_ref[j, 1] = v_ref[pl.ds(row, PAGE), :]
        start = pl.multiple_of(first_ref[0], PAGE)
        keys = k_ref[pl.ds(start, span), :]
        values = v_ref[pl.ds(start, span), :]
        qs = qs_ref[...]
        live = qs < docs - 1
        allowed = (ks_ref[...] == qs) & (kp_ref[...] <= qp_ref[...]) & live
        for g in range(group):
            q = q_ref[:, g * HEAD:(g + 1) * HEAD]
            scores = lax.dot_general(
                q, keys, (((1,), (1,)), ((), ())), preferred_element_type=jnp.float32
            ) * scale
            scores = jnp.where(allowed, scores, neg_large)
            top = jnp.max(scores, axis=1, keepdims=True)
            expo = jnp.exp(scores - top)
            denom = jnp.sum(expo, axis=1, keepdims=True)
            acc = jnp.dot(expo.astype(jnp.bfloat16), values, preferred_element_type=jnp.float32)
            out = jnp.where(live, acc / jnp.where(live, denom, 1.0), 0.0)
            o_ref[:, g * HEAD:(g + 1) * HEAD] = out.astype(o_ref.dtype)

    spec = pltpu.PrefetchScalarGridSpec(
        num_scalar_prefetch=2,
        grid=(kv_dev,),
        in_specs=[
            pl.BlockSpec((rows, group * HEAD), lambda c, f, p: (0, c)),
            pl.BlockSpec((count, HEAD), lambda c, f, p: (0, c)),
            pl.BlockSpec((count, HEAD), lambda c, f, p: (0, kv_dev + c)),
            pl.BlockSpec((rows, 1), lambda c, f, p: (0, 0)),
            pl.BlockSpec((rows, 1), lambda c, f, p: (0, 0)),
            pl.BlockSpec((1, span), lambda c, f, p: (0, 0)),
            pl.BlockSpec((1, span), lambda c, f, p: (0, 0)),
        ],
        out_specs=[
            pl.BlockSpec((rows, group * HEAD), lambda c, f, p: (0, c)),
            pl.BlockSpec((slots, 2, PAGE, HEAD), lambda c, f, p: (0, 0, 0, c)),
        ],
    )
    return pl.pallas_call(
        kernel,
        grid_spec=spec,
        out_shape=[
            jax.ShapeDtypeStruct((rows, q_width), jnp.bfloat16),
            jax.ShapeDtypeStruct((slots, 2, PAGE, kv_dev * HEAD), both.dtype),
        ],
        interpret=interpret,
    )(
        first.reshape(1).astype(jnp.int32),
        pages.astype(jnp.int32),
        query,
        both,
        both,
        q_seg.reshape(rows, 1),
        q_pos.reshape(rows, 1),
        k_seg.reshape(1, span),
        k_pos.reshape(1, span),
    )

def on_device(
    tokens,
    norm_gain,
    w_query,
    w_key,
    w_value,
    query_bias,
    key_bias,
    value_bias,
    lengths,
    page_table,
):
    rows = tokens.shape[0]
    blocks = lax.axis_size("blk")
    me = lax.axis_index("blk")
    q_width = w_query.shape[1]
    kv_width = w_key.shape[1]
    kv_dev = kv_width // HEAD
    group = HEADS // KV_HEADS
    slots = rows // PAGE
    docs = lengths.shape[0]
    scale = 1.0 / float(HEAD) ** 0.5
    wide = tokens.astype(jnp.float32)
    scaled = (wide * norm_gain.astype(jnp.float32)).astype(jnp.bfloat16)
    part_sq = jnp.sum(wide * wide, axis=1)
    parts = lax.axis_size("tp")
    squares = part_sq
    for flip, perm in partners(parts):
        squares = squares + lax.ppermute(part_sq, "tp", perm)
    w_kv = jnp.concatenate([w_key, w_value], axis=1)
    width = tokens.shape[1]
    mine = lax.axis_index("tp")

    def project(chunk, source):
        return [
            jnp.dot(
                chunk,
                lax.dynamic_slice_in_dim(weight, source * width, width, 0),
                preferred_element_type=jnp.float32,
            )
            for weight in (w_kv, w_query)
        ]

    piece = jnp.zeros((parts,) + scaled.shape, scaled.dtype)
    piece = lax.dynamic_update_slice_in_dim(piece, scaled[None], mine, 0)
    for flip, perm in partners(parts):
        got = lax.ppermute(scaled, "tp", perm)
        piece = lax.dynamic_update_slice_in_dim(piece, got[None], flip(mine), 0)
    piece = jnp.transpose(piece, (1, 0, 2)).reshape(rows, parts * width)
    proj_kv = jnp.dot(piece, w_kv, preferred_element_type=jnp.float32)
    proj_query = jnp.dot(piece, w_query, preferred_element_type=jnp.float32)
    proj_key = proj_kv[:, :kv_width]
    proj_value = proj_kv[:, kv_width:]
    rstd = lax.rsqrt(squares / D + norm_eps)
    own_pos = me * rows + jnp.arange(rows, dtype=jnp.int32)
    own_seg, own_off = token_meta(own_pos, lengths)
    own_live = own_seg < docs - 1
    query = rstd[:, None] * proj_query + query_bias.astype(jnp.float32)
    key = rstd[:, None] * proj_key + key_bias.astype(jnp.float32)
    value = rstd[:, None] * proj_value + value_bias.astype(jnp.float32)
    query = (
        rotate(query.reshape(rows, q_width // HEAD, HEAD), own_off)
        .reshape(rows, q_width)
        .astype(jnp.bfloat16)
    )
    key = (
        jnp.where(own_live[:, None, None], rotate(key.reshape(rows, kv_dev, HEAD), own_off), 0.0)
        .reshape(rows, kv_width)
        .astype(jnp.bfloat16)
    )
    value = jnp.where(own_live[:, None], value, 0.0).astype(jnp.bfloat16)
    q_seg, q_off = token_meta(own_pos, lengths)
    q_live = q_seg < docs - 1
    q_grouped = query.reshape(rows, kv_dev, group, HEAD)

    both = lax.all_gather(jnp.concatenate([key, value], axis=1), "blk", axis=0, tiled=True)
    count = both.shape[0]
    longest = count // 2
    span = min(count, longest + rows)
    first = jnp.clip(me * rows - longest, 0, count - span)
    k_pos = first + jnp.arange(span, dtype=jnp.int32)
    k_seg, k_off = token_meta(k_pos, lengths)
    numbers = jnp.arange(page_table.shape[0], dtype=jnp.int32)
    pages = jnp.stack(
        [jnp.sum(jnp.where(page_table == me * slots + j, numbers, 0)) for j in range(slots)]
    )
    pages = jnp.clip(pages, 0, count // PAGE - 1)
    mixed, kv_cache = window_attention(
        first, query, both, q_seg, own_pos, k_seg, k_pos, docs, pages
    )
    return (mixed, kv_cache)


def solution(mesh):
    in_specs = (
        P("blk", "tp"),
        P("tp"),
        P(None, "tp"),
        P(None, "tp"),
        P(None, "tp"),
        P("tp"),
        P("tp"),
        P("tp"),
        P(),
        P(),
    )
    out_specs = (P("blk", "tp"), P("blk", None, None, "tp"))
    return jax.shard_map(
        on_device, mesh=mesh, in_specs=in_specs, out_specs=out_specs, check_vma=False
    )
```

```python
import jax
import jax.numpy as jnp
from jax import lax
from jax.experimental import pallas as pl
from jax.experimental.pallas import tpu as pltpu
from jax.sharding import PartitionSpec as P

D = 5120
HEADS = 40
KV_HEADS = 8
HEAD = 128
PAGE = 128


rope_base = 1000000.0
norm_eps = 1e-06
neg_large = -1e30


def token_meta(positions, lengths):
    ends = jnp.cumsum(lengths)
    past = (positions[:, None] >= ends[None, :]).astype(jnp.int32)
    segment = jnp.sum(past, axis=1)
    start = jnp.sum(past * lengths[None, :], axis=1)
    return (segment, positions - start)


def rotate(values, offsets):
    half = HEAD // 2
    freq = rope_base ** (-2.0 * jnp.arange(half, dtype=jnp.float32) / HEAD)
    angle = offsets.astype(jnp.float32)[:, None] * freq[None, :]
    cosine = jnp.cos(angle)[:, None, :]
    sine = jnp.sin(angle)[:, None, :]
    first = values[..., :half]
    second = values[..., half:]
    return jnp.concatenate(
        [first * cosine - second * sine, second * cosine + first * sine], axis=-1
    )


def partners(size):
    if size & (size - 1) == 0:
        return [
            ((lambda i, s=s: jnp.bitwise_xor(i, s)), [(j, j ^ s) for j in range(size)])
            for s in range(1, size)
        ]
    return [
        ((lambda i, s=s: (i + size - s) % size), [(j, (j + s) % size) for j in range(size)])
        for s in range(1, size)
    ]

def window_attention(first, query, both, q_seg, q_pos, k_seg, k_pos, docs, pages, interpret=False):
    rows, q_width = query.shape
    count, both_width = both.shape
    span = k_seg.shape[0]
    kv_dev = both_width // (2 * HEAD)
    group = q_width // (kv_dev * HEAD)
    scale = 1.0 / float(HEAD) ** 0.5

    slots = pages.shape[0]

    def kernel(first_ref, page_ref, q_ref, k_ref, v_ref, qs_ref, ks_ref, o_ref, c_ref):
        for j in range(slots):
            row = pl.multiple_of(page_ref[j] * PAGE, PAGE)
            c_ref[j, 0] = k_ref[pl.ds(row, PAGE), :]
            c_ref[j, 1] = v_ref[pl.ds(row, PAGE), :]
        start = pl.multiple_of(first_ref[0], PAGE)
        keys = k_ref[pl.ds(start, span), :]
        values = v_ref[pl.ds(start, span), :]
        live = qs_ref[...] < docs - 1
        bias = ks_ref[...].astype(jnp.float32)
        for g in range(group):
            q = q_ref[:, g * HEAD:(g + 1) * HEAD]
            scores = lax.dot_general(
                q, keys, (((1,), (1,)), ((), ())), preferred_element_type=jnp.float32
            ) * scale
            scores = scores + bias
            top = jnp.max(scores, axis=1, keepdims=True)
            expo = jnp.exp(scores - top)
            denom = jnp.sum(expo, axis=1, keepdims=True)
            acc = jnp.dot(expo.astype(jnp.bfloat16), values, preferred_element_type=jnp.float32)
            out = jnp.where(live, acc / jnp.where(live, denom, 1.0), 0.0)
            o_ref[:, g * HEAD:(g + 1) * HEAD] = out.astype(o_ref.dtype)

    spec = pltpu.PrefetchScalarGridSpec(
        num_scalar_prefetch=2,
        grid=(kv_dev,),
        in_specs=[
            pl.BlockSpec((rows, group * HEAD), lambda c, f, p: (0, c)),
            pl.BlockSpec((count, HEAD), lambda c, f, p: (0, c)),
            pl.BlockSpec((count, HEAD), lambda c, f, p: (0, kv_dev + c)),
            pl.BlockSpec((rows, 1), lambda c, f, p: (0, 0)),
            pl.BlockSpec((rows, span), lambda c, f, p: (0, 0)),
        ],
        out_specs=[
            pl.BlockSpec((rows, group * HEAD), lambda c, f, p: (0, c)),
            pl.BlockSpec((slots, 2, PAGE, HEAD), lambda c, f, p: (0, 0, 0, c)),
        ],
    )
    return pl.pallas_call(
        kernel,
        grid_spec=spec,
        out_shape=[
            jax.ShapeDtypeStruct((rows, q_width), jnp.bfloat16),
            jax.ShapeDtypeStruct((slots, 2, PAGE, kv_dev * HEAD), both.dtype),
        ],
        interpret=interpret,
    )(
        first.reshape(1).astype(jnp.int32),
        pages.astype(jnp.int32),
        query,
        both,
        both,
        q_seg.reshape(rows, 1),
        jnp.where(
            (k_seg[None, :] == q_seg[:, None])
            & (k_pos[None, :] <= q_pos[:, None])
            & (q_seg[:, None] < docs - 1),
            0.0,
            neg_large,
        ).astype(jnp.bfloat16),
    )

def on_device(
    tokens,
    norm_gain,
    w_query,
    w_key,
    w_value,
    query_bias,
    key_bias,
    value_bias,
    lengths,
    page_table,
):
    rows = tokens.shape[0]
    blocks = lax.axis_size("blk")
    me = lax.axis_index("blk")
    q_width = w_query.shape[1]
    kv_width = w_key.shape[1]
    kv_dev = kv_width // HEAD
    group = HEADS // KV_HEADS
    slots = rows // PAGE
    docs = lengths.shape[0]
    scale = 1.0 / float(HEAD) ** 0.5
    wide = tokens.astype(jnp.float32)
    scaled = (wide * norm_gain.astype(jnp.float32)).astype(jnp.bfloat16)
    part_sq = jnp.sum(wide * wide, axis=1)
    parts = lax.axis_size("tp")
    squares = part_sq
    for flip, perm in partners(parts):
        squares = squares + lax.ppermute(part_sq, "tp", perm)
    w_kv = jnp.concatenate([w_key, w_value], axis=1)
    width = tokens.shape[1]
    mine = lax.axis_index("tp")

    def project(chunk, source):
        return [
            jnp.dot(
                chunk,
                lax.dynamic_slice_in_dim(weight, source * width, width, 0),
                preferred_element_type=jnp.float32,
            )
            for weight in (w_kv, w_query)
        ]

    proj_kv, proj_query = project(scaled, mine)
    for flip, perm in partners(parts):
        got = lax.ppermute(scaled, "tp", perm)
        more = project(got, flip(mine))
        proj_kv = proj_kv + more[0]
        proj_query = proj_query + more[1]
    proj_key = proj_kv[:, :kv_width]
    proj_value = proj_kv[:, kv_width:]
    rstd = lax.rsqrt(squares / D + norm_eps)
    own_pos = me * rows + jnp.arange(rows, dtype=jnp.int32)
    own_seg, own_off = token_meta(own_pos, lengths)
    own_live = own_seg < docs - 1
    query = rstd[:, None] * proj_query + query_bias.astype(jnp.float32)
    key = rstd[:, None] * proj_key + key_bias.astype(jnp.float32)
    value = rstd[:, None] * proj_value + value_bias.astype(jnp.float32)
    query = (
        rotate(query.reshape(rows, q_width // HEAD, HEAD), own_off)
        .reshape(rows, q_width)
        .astype(jnp.bfloat16)
    )
    key = (
        jnp.where(own_live[:, None, None], rotate(key.reshape(rows, kv_dev, HEAD), own_off), 0.0)
        .reshape(rows, kv_width)
        .astype(jnp.bfloat16)
    )
    value = jnp.where(own_live[:, None], value, 0.0).astype(jnp.bfloat16)
    q_seg, q_off = token_meta(own_pos, lengths)
    q_live = q_seg < docs - 1
    q_grouped = query.reshape(rows, kv_dev, group, HEAD)

    both = lax.all_gather(jnp.concatenate([key, value], axis=1), "blk", axis=0, tiled=True)
    count = both.shape[0]
    longest = count // 2
    span = min(count, longest + rows)
    first = jnp.clip(me * rows - longest, 0, count - span)
    k_pos = first + jnp.arange(span, dtype=jnp.int32)
    k_seg, k_off = token_meta(k_pos, lengths)
    numbers = jnp.arange(page_table.shape[0], dtype=jnp.int32)
    pages = jnp.stack(
        [jnp.sum(jnp.where(page_table == me * slots + j, numbers, 0)) for j in range(slots)]
    )
    pages = jnp.clip(pages, 0, count // PAGE - 1)
    mixed, kv_cache = window_attention(
        first, query, both, q_seg, own_pos, k_seg, k_pos, docs, pages
    )
    return (mixed, kv_cache)


def solution(mesh):
    in_specs = (
        P("blk", "tp"),
        P("tp"),
        P(None, "tp"),
        P(None, "tp"),
        P(None, "tp"),
        P("tp"),
        P("tp"),
        P("tp"),
        P(),
        P(),
    )
    out_specs = (P("blk", "tp"), P("blk", None, None, "tp"))
    return jax.shard_map(
        on_device, mesh=mesh, in_specs=in_specs, out_specs=out_specs, check_vma=False
    )
```

```python
import jax
import jax.numpy as jnp
from jax import lax
from jax.experimental import pallas as pl
from jax.experimental.pallas import tpu as pltpu
from jax.sharding import PartitionSpec as P

D = 5120
HEADS = 40
KV_HEADS = 8
HEAD = 128
PAGE = 128


rope_base = 1000000.0
norm_eps = 1e-06
neg_large = -1e30


def token_meta(positions, lengths):
    ends = jnp.cumsum(lengths)
    past = (positions[:, None] >= ends[None, :]).astype(jnp.int32)
    segment = jnp.sum(past, axis=1)
    start = jnp.sum(past * lengths[None, :], axis=1)
    return (segment, positions - start)


def rotate(values, offsets):
    half = HEAD // 2
    freq = rope_base ** (-2.0 * jnp.arange(half, dtype=jnp.float32) / HEAD)
    angle = offsets.astype(jnp.float32)[:, None] * freq[None, :]
    cosine = jnp.cos(angle)[:, None, :]
    sine = jnp.sin(angle)[:, None, :]
    first = values[..., :half]
    second = values[..., half:]
    return jnp.concatenate(
        [first * cosine - second * sine, second * cosine + first * sine], axis=-1
    )


def partners(size):
    if size & (size - 1) == 0:
        return [
            ((lambda i, s=s: jnp.bitwise_xor(i, s)), [(j, j ^ s) for j in range(size)])
            for s in range(1, size)
        ]
    return [
        ((lambda i, s=s: (i + size - s) % size), [(j, (j + s) % size) for j in range(size)])
        for s in range(1, size)
    ]

def window_attention(first, query, both, q_seg, q_pos, k_seg, k_pos, docs, pages, interpret=False):
    rows, q_width = query.shape
    count, both_width = both.shape
    span = k_seg.shape[0]
    kv_dev = both_width // (2 * HEAD)
    group = q_width // (kv_dev * HEAD)
    scale = 1.0 / float(HEAD) ** 0.5

    slots = pages.shape[0]

    def kernel(first_ref, page_ref, q_ref, k_ref, v_ref, qs_ref, ks_ref, o_ref, c_ref):
        for j in range(slots):
            row = pl.multiple_of(page_ref[j] * PAGE, PAGE)
            c_ref[j, 0] = k_ref[pl.ds(row, PAGE), :]
            c_ref[j, 1] = v_ref[pl.ds(row, PAGE), :]
        start = pl.multiple_of(first_ref[0], PAGE)
        keys = k_ref[pl.ds(start, span), :]
        values = v_ref[pl.ds(start, span), :]
        live = qs_ref[...] < docs - 1
        bias = ks_ref[...].astype(jnp.float32)
        for g in range(group):
            q = q_ref[:, g * HEAD:(g + 1) * HEAD]
            scores = lax.dot_general(
                q, keys, (((1,), (1,)), ((), ())), preferred_element_type=jnp.float32
            )
            scores = scores + bias
            top = jnp.max(scores, axis=1, keepdims=True)
            expo = jnp.exp((scores - top) * scale)
            denom = jnp.sum(expo, axis=1, keepdims=True)
            acc = jnp.dot(expo.astype(jnp.bfloat16), values, preferred_element_type=jnp.float32)
            out = jnp.where(live, acc / jnp.where(live, denom, 1.0), 0.0)
            o_ref[:, g * HEAD:(g + 1) * HEAD] = out.astype(o_ref.dtype)

    spec = pltpu.PrefetchScalarGridSpec(
        num_scalar_prefetch=2,
        grid=(kv_dev,),
        in_specs=[
            pl.BlockSpec((rows, group * HEAD), lambda c, f, p: (0, c)),
            pl.BlockSpec((count, HEAD), lambda c, f, p: (0, c)),
            pl.BlockSpec((count, HEAD), lambda c, f, p: (0, kv_dev + c)),
            pl.BlockSpec((rows, 1), lambda c, f, p: (0, 0)),
            pl.BlockSpec((rows, span), lambda c, f, p: (0, 0)),
        ],
        out_specs=[
            pl.BlockSpec((rows, group * HEAD), lambda c, f, p: (0, c)),
            pl.BlockSpec((slots, 2, PAGE, HEAD), lambda c, f, p: (0, 0, 0, c)),
        ],
    )
    return pl.pallas_call(
        kernel,
        grid_spec=spec,
        out_shape=[
            jax.ShapeDtypeStruct((rows, q_width), jnp.bfloat16),
            jax.ShapeDtypeStruct((slots, 2, PAGE, kv_dev * HEAD), both.dtype),
        ],
        interpret=interpret,
    )(
        first.reshape(1).astype(jnp.int32),
        pages.astype(jnp.int32),
        query,
        both,
        both,
        q_seg.reshape(rows, 1),
        jnp.where(
            (k_seg[None, :] == q_seg[:, None])
            & (k_pos[None, :] <= q_pos[:, None])
            & (q_seg[:, None] < docs - 1),
            0.0,
            neg_large,
        ).astype(jnp.bfloat16),
    )

def on_device(
    tokens,
    norm_gain,
    w_query,
    w_key,
    w_value,
    query_bias,
    key_bias,
    value_bias,
    lengths,
    page_table,
):
    rows = tokens.shape[0]
    blocks = lax.axis_size("blk")
    me = lax.axis_index("blk")
    q_width = w_query.shape[1]
    kv_width = w_key.shape[1]
    kv_dev = kv_width // HEAD
    group = HEADS // KV_HEADS
    slots = rows // PAGE
    docs = lengths.shape[0]
    scale = 1.0 / float(HEAD) ** 0.5
    wide = tokens.astype(jnp.float32)
    scaled = (wide * norm_gain.astype(jnp.float32)).astype(jnp.bfloat16)
    part_sq = jnp.sum(wide * wide, axis=1)
    parts = lax.axis_size("tp")
    squares = part_sq
    for flip, perm in partners(parts):
        squares = squares + lax.ppermute(part_sq, "tp", perm)
    w_kv = jnp.concatenate([w_key, w_value], axis=1)
    width = tokens.shape[1]
    mine = lax.axis_index("tp")

    def project(chunk, source):
        return [
            jnp.dot(
                chunk,
                lax.dynamic_slice_in_dim(weight, source * width, width, 0),
                preferred_element_type=jnp.float32,
            )
            for weight in (w_kv, w_query)
        ]

    proj_kv, proj_query = project(scaled, mine)
    for flip, perm in partners(parts):
        got = lax.ppermute(scaled, "tp", perm)
        more = project(got, flip(mine))
        proj_kv = proj_kv + more[0]
        proj_query = proj_query + more[1]
    proj_key = proj_kv[:, :kv_width]
    proj_value = proj_kv[:, kv_width:]
    rstd = lax.rsqrt(squares / D + norm_eps)
    own_pos = me * rows + jnp.arange(rows, dtype=jnp.int32)
    own_seg, own_off = token_meta(own_pos, lengths)
    own_live = own_seg < docs - 1
    query = rstd[:, None] * proj_query + query_bias.astype(jnp.float32)
    key = rstd[:, None] * proj_key + key_bias.astype(jnp.float32)
    value = rstd[:, None] * proj_value + value_bias.astype(jnp.float32)
    query = (
        rotate(query.reshape(rows, q_width // HEAD, HEAD), own_off)
        .reshape(rows, q_width)
        .astype(jnp.bfloat16)
    )
    key = (
        jnp.where(own_live[:, None, None], rotate(key.reshape(rows, kv_dev, HEAD), own_off), 0.0)
        .reshape(rows, kv_width)
        .astype(jnp.bfloat16)
    )
    value = jnp.where(own_live[:, None], value, 0.0).astype(jnp.bfloat16)
    q_seg, q_off = token_meta(own_pos, lengths)
    q_live = q_seg < docs - 1
    q_grouped = query.reshape(rows, kv_dev, group, HEAD)

    both = lax.all_gather(jnp.concatenate([key, value], axis=1), "blk", axis=0, tiled=True)
    count = both.shape[0]
    longest = count // 2
    span = min(count, longest + rows)
    first = jnp.clip(me * rows - longest, 0, count - span)
    k_pos = first + jnp.arange(span, dtype=jnp.int32)
    k_seg, k_off = token_meta(k_pos, lengths)
    numbers = jnp.arange(page_table.shape[0], dtype=jnp.int32)
    pages = jnp.stack(
        [jnp.sum(jnp.where(page_table == me * slots + j, numbers, 0)) for j in range(slots)]
    )
    pages = jnp.clip(pages, 0, count // PAGE - 1)
    mixed, kv_cache = window_attention(
        first, query, both, q_seg, own_pos, k_seg, k_pos, docs, pages
    )
    return (mixed, kv_cache)


def solution(mesh):
    in_specs = (
        P("blk", "tp"),
        P("tp"),
        P(None, "tp"),
        P(None, "tp"),
        P(None, "tp"),
        P("tp"),
        P("tp"),
        P("tp"),
        P(),
        P(),
    )
    out_specs = (P("blk", "tp"), P("blk", None, None, "tp"))
    return jax.shard_map(
        on_device, mesh=mesh, in_specs=in_specs, out_specs=out_specs, check_vma=False
    )
```
